32 devices in a mesh: dp: 32 (over z, y, x, core), mp: 1.
Axes of the slice: x: 2, y: 2, z: 4, core: 2. Of those that a mesh axis runs over, the one named last changes fastest.
Arguments:
- pre_tokens: bfloat16 [16384, 1024], P(('dp', 'mp')), may hold values from -6 to 6
- dec_tokens: bfloat16 [128, 1024], P(('dp', 'mp')), may hold values from -6 to 6
- deal_slots: int32 [128], replicated, may hold values from 0 to 127, as said below
- dec_lengths: int32 [128], P('dp'), may hold values from 1 to 256, as said below
- pre_offsets: int32 [32], P('dp'), may hold values from 0 to 1024, as said below
- dec_cache: bfloat16 [8, 128, 256, 128], P('mp', 'dp'), may hold values from -420 to 420, as said below
- prior_cache: bfloat16 [8, 32, 1024, 128], P('mp', 'dp'), may hold values from -420 to 420, as said below
- attn_gain: float32 [1024], replicated, may hold values from 0.5 to 2
- moe_gain: float32 [1024], replicated, may hold values from 0.5 to 2
- qkv_weight: bfloat16 [1024, 2048], P('dp', 'mp'), may hold values from -0.1875 to 0.1875
- out_weight: bfloat16 [1024, 1024], P('mp', 'dp'), may hold values from -0.1875 to 0.1875
- gate_up: bfloat16 [32, 1024, 1024], P(None, 'dp', 'mp'), may hold values from -0.1875 to 0.1875
- down_weight: bfloat16 [32, 512, 1024], P(None, 'dp', 'mp'), may hold values from -0.25 to 0.25
- routes: int32 [16512, 8], P(('dp', 'mp')), may hold values from 0 to 31, all different within a row; in each aligned block of 516 rows (0 to 515, 516 to 1031, ...) at most 172 rows name the same one
- route_gates: bfloat16 [16512, 8], P(('dp', 'mp')), may hold values from 0.019897461 to 0.29882812
Outputs:
- hidden: bfloat16 [16512, 1024], P(('dp', 'mp'))
The draws below stay inside these ranges and needn't reach their ends.
Inputs may be any that keep to these rules, and one draw needn't show every extreme that they name: deal_slots is a permutation of the decode slots; a request keeps its index in mp and its position among the 4 requests of a device; the positions of one device form aligned blocks of 1 that go to one group each, different blocks to different groups. `dec_lengths`: in every draw some slot has exactly 256 cached positions. `pre_offsets`: in every draw some group has exactly 1024 cached positions before its prefill tokens. `dec_cache`: keys hold the first 64 entries of the last dimension, values the rest. `prior_cache`: keys hold the first 64 entries of the last dimension, values the rest. `routes`: each row names 8 different experts; within the 516 rows of one device no expert is named by more than 172 rows, a bound that some block reaches.
All inputs are finite; a program needn't handle non-finite values.
Results may differ from the reference program's by a relative error of at most 0.019.
Values may be sent and summed in bfloat16 or wider, within the bound.
No kernel may reach another device: no remote copies, remote signals or barrier semaphores. Data moves between devices by JAX's collectives and lax.ppermute only.
A program may use at most 128 MiB of HBM per device.

```python
import math
import jax
import jax.numpy as jnp
import numpy as np
from jax import lax

D = 1024
HEADS = 16
KVH = 8
HD = 64
EXP = 32
FF = 512
TOPK = 8
PRE_LEN = 512
DEC_DEV = 4
CACHE = 256
PRIOR = 1024
ROWS_DEV = 516
CAP = 172
BUNDLE = 1
DECODE = 128
ROWS_ALL = 16512
GW = 256
N_DP = 32
N_MP = 1


def cache_values(key, shape):
    key_part, value_part = jax.random.split(key, 2)
    half_shape = shape[:-1] + (shape[-1] // 2,)
    key_rows = jax.random.truncated_normal(key_part, -6.0, 6.0, half_shape, jnp.float32) * 8.0
    value_rows = jax.random.truncated_normal(value_part, -6.0, 6.0, half_shape, jnp.float32) * 4.0
    return jnp.concatenate([key_rows, value_rows], axis=-1)


def draw_dec_cache(key, part):
    return cache_values(jax.random.fold_in(key, 11), (KVH, DECODE, CACHE, 2 * HD)).astype(jnp.bfloat16)


def draw_prior_cache(key, part):
    return cache_values(jax.random.fold_in(key, 13), (KVH, N_DP, PRIOR, 2 * HD)).astype(jnp.bfloat16)


def draw_deal_slots(key, part):
    first_key, second_key = jax.random.split(jax.random.fold_in(key, 17))
    block_count = DEC_DEV // BUNDLE
    group_order = jax.random.permutation(first_key, N_DP)
    block_shift = jax.random.permutation(second_key, N_DP)[:block_count]
    group_ids = jnp.arange(N_DP)[:, None, None]
    part_ids = jnp.arange(N_MP)[None, :, None]
    position = jnp.arange(DEC_DEV)[None, None, :]
    target = (group_order[group_ids] + block_shift[position // BUNDLE]) % N_DP
    slot_ids = (target * N_MP + part_ids) * DEC_DEV + position
    return slot_ids.reshape(-1).astype(jnp.int32)


def draw_dec_lengths(key, part):
    first_key, second_key, third_key = jax.random.split(jax.random.fold_in(key, 19), 3)
    longer = jax.random.randint(first_key, (DECODE,), 1, CACHE + 1)
    shorter = jax.random.randint(second_key, (DECODE,), 1, CACHE + 1)
    chosen = jax.random.randint(third_key, (), 0, DECODE)
    lengths = jnp.minimum(longer, shorter)
    return jnp.where(jnp.arange(DECODE) == chosen, CACHE, lengths).astype(jnp.int32)


def draw_pre_offsets(key, part):
    first_key, second_key = jax.random.split(jax.random.fold_in(key, 23))
    offsets = jax.random.randint(first_key, (N_DP,), 0, PRIOR + 1)
    chosen = jax.random.randint(second_key, (), 0, N_DP)
    return jnp.where(jnp.arange(N_DP) == chosen, PRIOR, offsets).astype(jnp.int32)


def shard_levels(stream_key, dims, shards, least, high):
    def one(dim, shards_of):
        heights = jax.random.uniform(jax.random.fold_in(jax.random.fold_in(stream_key, 6), dim), (shards_of,), jnp.float32, least / len(shards), high / len(shards))
        return jnp.repeat(jnp.exp(heights), dims[dim] // shards_of).reshape((-1,) + (1,) * (len(dims) - dim - 1))

    loudness = one(*shards[0])
    for cut in shards[1:]:
        loudness = loudness * one(*cut)
    return loudness


def routed_block(stream_key, own, number, rows, amount, top, reach, slope):
    order = jax.random.permutation(stream_key, amount)
    heavy_load, ordinary = shares(amount, rows * top, reach, slope, True), shares(amount, rows * top, reach, slope, False)
    places = jnp.arange(amount)

    def named(sizes, turn):
        used = int((sizes > 0).sum())
        fixed = max(1, used // 4)
        passed = fixed + (places - fixed + turn * (used - fixed)) % max(1, amount - fixed)
        return jnp.zeros((amount,), jnp.int32).at[order[jnp.where(places < fixed, places, passed)]].set(jnp.asarray(sizes, jnp.int32))

    sizes = jnp.where(number % 4 == 0, named(heavy_load, number // 4), named(ordinary, number - number // 4 - 1))
    mixed = jax.random.permutation(jax.random.fold_in(own, 3), amount)
    source_of, sink = mixed[0:amount // 2 * 2:2], mixed[1:amount // 2 * 2:2]
    margin = jnp.minimum(sizes[source_of] - 1, reach - sizes[sink]) // 2
    margin = jnp.where((source_of == order[0]) | (sink == order[0]) | (sizes[sink] == 0), 0, jnp.maximum(margin, 0))
    passed = jax.random.randint(jax.random.fold_in(own, 4), (amount // 2,), 0, 1 << 20) % (margin + 1)
    sizes = sizes.at[source_of].add(-passed).at[sink].add(passed)
    labels = jnp.searchsorted(jnp.cumsum(sizes), jnp.arange(rows * top), side="right").astype(jnp.int32)
    listing = labels.reshape(top, rows).T
    listing = listing[jax.random.permutation(jax.random.fold_in(own, 1), rows)]
    turn = jax.random.randint(jax.random.fold_in(own, 2), (rows, 1), 0, top)
    return jnp.take_along_axis(listing, (jnp.arange(top)[None, :] + turn) % top, axis=1)


def shares(amount, total, reach, lean, full):
    loads = [(1 << 20) // math.isqrt(grade ** lean) + 1 for grade in range(1, amount + 1)]
    largest = reach if full else min(reach, max(-(-total // amount), total * loads[0] // sum(loads)))
    least = 1 if total - largest >= amount - 1 else 0
    counts, spare = [largest] + [least] * (amount - 1), total - largest - least * (amount - 1)
    while spare > 0:
        movable = [i for i in range(1, amount) if counts[i] < largest] or [i for i in range(1, amount) if counts[i] < reach]
        pool, remaining = sum([loads[i] for i in movable]), spare
        for i in movable:
            addition = min(reach - counts[i], max(1, remaining * loads[i] // pool), spare)
            counts[i] = counts[i] + addition
            spare = spare - addition
    return np.array(counts)


def noise(own_key, dims, spread, reach, cuts=(), kind=jnp.bfloat16):
    values = spread * jax.random.normal(own_key, dims, jnp.float32)
    if cuts:
        values = values * shard_levels(own_key, dims, cuts, -0.22, 0.18)
    return jnp.clip(values, -reach, reach).astype(kind)


def setup_inputs(seed: int = 0) -> dict:
    keys = jax.random.split(jax.random.key(seed), 16)
    pre_tokens = noise(keys[0], (N_DP * PRE_LEN, D), 1.0, 6.0, ((0, 32),))
    dec_tokens = noise(keys[1], (DECODE, D), 1.0, 6.0, ((0, 32),))
    deal_slots = draw_deal_slots(jax.random.fold_in(keys[15], 71), 0)
    dec_lengths = draw_dec_lengths(jax.random.fold_in(keys[15], 71), 0)
    pre_offsets = draw_pre_offsets(jax.random.fold_in(keys[15], 71), 0)
    dec_cache = draw_dec_cache(jax.random.fold_in(keys[15], 71), 0)
    prior_cache = draw_prior_cache(jax.random.fold_in(keys[15], 71), 0)
    attn_gain = jnp.clip(jnp.exp(jax.random.uniform(keys[7], (D,), jnp.float32, math.log(0.5), math.log(2.0))), 0.5, 2.0)
    moe_gain = jnp.clip(jnp.exp(jax.random.uniform(keys[8], (D,), jnp.float32, math.log(0.5), math.log(2.0))), 0.5, 2.0)
    qkv_weight = noise(keys[9], (D, KVH * GW), D ** -0.5, 0.1875, ((0, 32),))
    out_weight = noise(keys[10], (HEADS * HD, D), (HEADS * HD) ** -0.5, 0.1875, ((1, 32),))
    gate_up = noise(keys[11], (EXP, D, 2 * FF), D ** -0.5, 0.1875, ((1, 32),))
    down_weight = noise(keys[12], (EXP, FF, D), FF ** -0.5, 0.25, ((1, 32),))
    routes_keys = jax.random.split(jax.random.fold_in(keys[13], 1), ROWS_ALL // ROWS_DEV)
    routes_turns = jax.random.permutation(jax.random.fold_in(keys[13], 3), ROWS_ALL // ROWS_DEV)
    routes = jax.vmap(lambda own, number: routed_block(jax.random.fold_in(keys[13], 2), own, number, ROWS_DEV, EXP, TOPK, CAP, 1))(routes_keys, routes_turns).reshape((ROWS_ALL, TOPK))
    route_gates = jnp.clip(0.019897461 + 0.27893066 * jax.random.uniform(keys[14], (ROWS_ALL, TOPK), jnp.float32) ** shard_levels(keys[14], (ROWS_ALL, TOPK), ((0, 32),), -0.2, 0.2), 0.019897461, 0.29882812).astype(jnp.bfloat16)
    return dict(pre_tokens=pre_tokens, dec_tokens=dec_tokens, deal_slots=deal_slots, dec_lengths=dec_lengths, pre_offsets=pre_offsets, dec_cache=dec_cache, prior_cache=prior_cache, attn_gain=attn_gain, moe_gain=moe_gain, qkv_weight=qkv_weight, out_weight=out_weight, gate_up=gate_up, down_weight=down_weight, routes=routes, route_gates=route_gates)


EPSILON = 1e-06
ROTARY_BASE = 10000.0
SCORE_SCALE = 0.015625

def root_norm(values, gain):
    mean_square = lax.optimization_barrier(jnp.mean(values * values, axis=-1, keepdims=True))
    return values * lax.rsqrt(mean_square + EPSILON) * gain

def rotary(vectors, positions):
    halfway = vectors.shape[-1] // 2
    freq_table = ROTARY_BASE ** (-jnp.arange(halfway).astype(jnp.float32) / halfway)
    angles = positions[..., None] * freq_table
    cosine = jnp.cos(angles)
    sine_part = jnp.sin(angles)
    leading = vectors[..., :halfway]
    trailing = vectors[..., halfway:]
    return jnp.concatenate([leading * cosine - trailing * sine_part, trailing * cosine + leading * sine_part], axis=-1)

def split_heads(projected, positions, head_dim):
    per_group = projected.shape[-1] // head_dim - 2
    row_count = projected.shape[0]
    group_count = projected.shape[1]
    queries = projected[..., :per_group * head_dim].reshape(row_count, group_count, per_group, head_dim)
    key_rows = projected[..., per_group * head_dim:(per_group + 1) * head_dim]
    value_rows = projected[..., (per_group + 1) * head_dim:]
    queries = rotary(queries, positions[:, None, None]).astype(jnp.bfloat16)
    key_rows = rotary(key_rows, positions[:, None]).astype(jnp.bfloat16)
    return (queries, key_rows, value_rows.astype(jnp.bfloat16))

def prefill_attention(queries, key_rows, value_rows, prior, offset):
    head_dim = queries.shape[-1]
    row_count = queries.shape[0]
    span = prior.shape[1]
    all_keys = jnp.concatenate([prior[:, :, :head_dim], jnp.swapaxes(key_rows, 0, 1)], axis=1)
    all_values = jnp.concatenate([prior[:, :, head_dim:], jnp.swapaxes(value_rows, 0, 1)], axis=1)
    scores = jnp.einsum('cgph,gkh->gpck', queries.astype(jnp.float32), all_keys.astype(jnp.float32)) * SCORE_SCALE
    column = jnp.arange(span + row_count)
    row_ids = jnp.arange(row_count)
    allowed = jnp.where(column[None, :] < span, column[None, :] < offset, column[None, :] - span <= row_ids[:, None])
    scores = jnp.where(allowed, scores, -jnp.inf)
    highest = lax.optimization_barrier(jnp.max(scores, axis=-1, keepdims=True))
    expo = jnp.exp(scores - highest)
    weights = (expo / lax.optimization_barrier(jnp.sum(expo, axis=-1, keepdims=True))).astype(jnp.bfloat16)
    mixed = jnp.einsum('gpck,gkh->cgph', weights.astype(jnp.float32), all_values.astype(jnp.float32))
    return mixed.astype(jnp.bfloat16)

def decode_attention(queries, key_rows, value_rows, cache, lengths):
    head_dim = queries.shape[-1]
    query_f = queries.astype(jnp.float32)
    cached = jnp.einsum('sgph,gslh->sgpl', query_f, cache[..., :head_dim].astype(jnp.float32)) * SCORE_SCALE
    own_score = jnp.einsum('sgph,sgh->sgp', query_f, key_rows.astype(jnp.float32)) * SCORE_SCALE
    valid = jnp.arange(cache.shape[2])[None, :] < lengths[:, None]
    cached = jnp.where(valid[:, None, None, :], cached, -jnp.inf)
    highest = jnp.maximum(lax.optimization_barrier(jnp.max(cached, axis=-1)), own_score)
    expo = jnp.exp(cached - highest[..., None])
    own_expo = jnp.exp(own_score - highest)
    total = lax.optimization_barrier(jnp.sum(expo, axis=-1)) + own_expo
    weights = (expo / total[..., None]).astype(jnp.bfloat16)
    own_weight = (own_expo / total).astype(jnp.bfloat16)
    mixed = jnp.einsum('sgpl,gslh->sgph', weights.astype(jnp.float32), cache[..., head_dim:].astype(jnp.float32))
    mixed = mixed + own_weight.astype(jnp.float32)[..., None] * value_rows.astype(jnp.float32)[:, :, None, :]
    return mixed.astype(jnp.bfloat16)

def group_attention(projected, prior, cache, lengths, offset, pre_rows, head_dim):
    part_count = projected.shape[0]
    pre_part = projected[:, :pre_rows].reshape((-1,) + projected.shape[2:])
    dec_part = projected[:, pre_rows:].reshape((-1,) + projected.shape[2:])
    pre_pos = (offset + jnp.arange(pre_part.shape[0], dtype=jnp.int32)).astype(jnp.float32)
    dec_pos = lengths.astype(jnp.float32)
    queries, key_rows, value_rows = split_heads(pre_part, pre_pos, head_dim)
    pre_out = prefill_attention(queries, key_rows, value_rows, prior, offset)
    queries, key_rows, value_rows = split_heads(dec_part, dec_pos, head_dim)
    dec_out = decode_attention(queries, key_rows, value_rows, cache, lengths)
    columns = pre_out.shape[1] * pre_out.shape[2] * pre_out.shape[3]
    pre_out = pre_out.reshape(part_count, pre_rows, columns)
    dec_out = dec_out.reshape(part_count, -1, columns)
    return jnp.concatenate([pre_out, dec_out], axis=1).reshape(-1, columns)

def reference(pre_tokens, dec_tokens, deal_slots, dec_lengths, pre_offsets, dec_cache, prior_cache, attn_gain, moe_gain, qkv_weight, out_weight, gate_up, down_weight, routes, route_gates):
    slot_rows = jnp.zeros_like(dec_tokens).at[deal_slots].set(dec_tokens)
    device_count = N_DP * N_MP
    pre_dev = PRE_LEN // N_MP
    rows_dev = pre_dev + DEC_DEV
    layer_input = jnp.concatenate([pre_tokens.reshape(device_count, pre_dev, D), slot_rows.reshape(device_count, DEC_DEV, D)], axis=1).reshape(-1, D)
    normed = root_norm(layer_input.astype(jnp.float32), attn_gain).astype(jnp.bfloat16)

    def group_step(group_index):
        group_rows = lax.dynamic_slice_in_dim(normed, group_index * N_MP * rows_dev, N_MP * rows_dev, 0)
        projected = jnp.dot(group_rows, qkv_weight, preferred_element_type=jnp.float32).reshape(N_MP, rows_dev, KVH, GW)
        prior = lax.dynamic_index_in_dim(prior_cache, group_index, 1, keepdims=False)
        cache = lax.dynamic_slice_in_dim(dec_cache, group_index * N_MP * DEC_DEV, N_MP * DEC_DEV, 1)
        lengths = lax.dynamic_slice_in_dim(dec_lengths, group_index * N_MP * DEC_DEV, N_MP * DEC_DEV, 0)
        offset = lax.dynamic_index_in_dim(pre_offsets, group_index, 0, keepdims=False)
        return group_attention(projected, prior, cache, lengths, offset, pre_dev, HD)
    attn_out = lax.map(group_step, jnp.arange(N_DP, dtype=jnp.int32)).reshape(-1, HEADS * HD)
    residual = layer_input.astype(jnp.float32) + jnp.dot(attn_out, out_weight, preferred_element_type=jnp.float32)
    normed_moe = root_norm(residual, moe_gain).astype(jnp.bfloat16)
    total_rows = normed_moe.shape[0]
    padded = jnp.concatenate([normed_moe, jnp.zeros((1, D), jnp.bfloat16)], axis=0)
    gates = route_gates.astype(jnp.float32)
    capacity = N_DP * N_MP * CAP

    def expert_step(running, expert):
        hits = routes == expert
        weight = lax.optimization_barrier(jnp.sum(jnp.where(hits, gates, 0.0), axis=1))
        chosen = jnp.nonzero(jnp.any(hits, axis=1), size=capacity, fill_value=total_rows)[0].astype(jnp.int32)
        picked = padded[chosen]
        both = jnp.dot(picked, gate_up[expert], preferred_element_type=jnp.float32)
        activation = (jax.nn.silu(both[:, :FF]) * both[:, FF:]).astype(jnp.bfloat16)
        expert_out = jnp.dot(activation, down_weight[expert], preferred_element_type=jnp.float32).astype(jnp.bfloat16)
        weight_pad = jnp.concatenate([weight, jnp.zeros((1,), jnp.float32)])[chosen]
        running = running.at[chosen].add(weight_pad[:, None] * expert_out.astype(jnp.float32), mode='drop')
        return (running, None)
    moe_sum, _ = lax.scan(expert_step, jnp.zeros((total_rows, D), jnp.float32), jnp.arange(EXP, dtype=jnp.int32))
    return (residual + moe_sum).astype(jnp.bfloat16)
```

```python
import jax
import jax.numpy as jnp
from jax import lax
from jax.sharding import PartitionSpec as P

EPSILON = 1e-06
ROTARY_BASE = 10000.0
SCORE_SCALE = 0.015625


def root_norm(values, gain):
    mean_square = jnp.mean(values * values, axis=-1, keepdims=True)
    return values * lax.rsqrt(mean_square + EPSILON) * gain


def rotary(vectors, positions):
    halfway = vectors.shape[-1] // 2
    freq_table = ROTARY_BASE ** (-jnp.arange(halfway).astype(jnp.float32) / halfway)
    angles = positions[..., None] * freq_table
    cosine = jnp.cos(angles)
    sine_part = jnp.sin(angles)
    leading = vectors[..., :halfway]
    trailing = vectors[..., halfway:]
    return jnp.concatenate(
        [leading * cosine - trailing * sine_part, trailing * cosine + leading * sine_part], axis=-1
    )


def split_heads(projected, positions, head_dim):
    per_group = projected.shape[-1] // head_dim - 2
    row_count = projected.shape[0]
    group_count = projected.shape[1]
    queries = projected[..., : per_group * head_dim].reshape(
        row_count, group_count, per_group, head_dim
    )
    key_rows = projected[..., per_group * head_dim : (per_group + 1) * head_dim]
    value_rows = projected[..., (per_group + 1) * head_dim :]
    queries = rotary(queries, positions[:, None, None]).astype(jnp.bfloat16)
    key_rows = rotary(key_rows, positions[:, None]).astype(jnp.bfloat16)
    return (queries, key_rows, value_rows.astype(jnp.bfloat16))


def prefill_attention(queries, key_rows, value_rows, prior, offset):
    head_dim = queries.shape[-1]
    row_count = queries.shape[0]
    span = prior.shape[1]
    all_keys = jnp.concatenate([prior[:, :, :head_dim], jnp.swapaxes(key_rows, 0, 1)], axis=1)
    all_values = jnp.concatenate([prior[:, :, head_dim:], jnp.swapaxes(value_rows, 0, 1)], axis=1)
    scores = (
        jnp.einsum("cgph,gkh->gpck", queries, all_keys, preferred_element_type=jnp.float32)
        * SCORE_SCALE
    )
    column = jnp.arange(span + row_count)
    row_ids = jnp.arange(row_count)
    allowed = jnp.where(
        column[None, :] < span, column[None, :] < offset, column[None, :] - span <= row_ids[:, None]
    )
    scores = jnp.where(allowed, scores, -jnp.inf)
    highest = jnp.max(scores, axis=-1, keepdims=True)
    expo = jnp.exp(scores - highest)
    weights = (expo / jnp.sum(expo, axis=-1, keepdims=True)).astype(jnp.bfloat16)
    mixed = jnp.einsum("gpck,gkh->cgph", weights, all_values, preferred_element_type=jnp.float32)
    return mixed.astype(jnp.bfloat16)


def decode_attention(queries, key_rows, value_rows, cache, lengths):
    head_dim = queries.shape[-1]
    cached = (
        jnp.einsum(
            "sgph,gslh->sgpl", queries, cache[..., :head_dim], preferred_element_type=jnp.float32
        )
        * SCORE_SCALE
    )
    own_score = (
        jnp.einsum("sgph,sgh->sgp", queries, key_rows, preferred_element_type=jnp.float32)
        * SCORE_SCALE
    )
    valid = jnp.arange(cache.shape[2])[None, :] < lengths[:, None]
    cached = jnp.where(valid[:, None, None, :], cached, -jnp.inf)
    highest = jnp.maximum(jnp.max(cached, axis=-1), own_score)
    expo = jnp.exp(cached - highest[..., None])
    own_expo = jnp.exp(own_score - highest)
    total = jnp.sum(expo, axis=-1) + own_expo
    weights = (expo / total[..., None]).astype(jnp.bfloat16)
    own_weight = (own_expo / total).astype(jnp.bfloat16)
    mixed = jnp.einsum(
        "sgpl,gslh->sgph", weights, cache[..., head_dim:], preferred_element_type=jnp.float32
    )
    mixed = (
        mixed
        + own_weight.astype(jnp.float32)[..., None] * value_rows.astype(jnp.float32)[:, :, None, :]
    )
    return mixed.astype(jnp.bfloat16)


def group_attention(projected, prior, cache, lengths, offset, pre_rows, head_dim):
    part_count = projected.shape[0]
    pre_part = projected[:, :pre_rows].reshape((-1,) + projected.shape[2:])
    dec_part = projected[:, pre_rows:].reshape((-1,) + projected.shape[2:])
    pre_pos = (offset + jnp.arange(pre_part.shape[0], dtype=jnp.int32)).astype(jnp.float32)
    dec_pos = lengths.astype(jnp.float32)
    queries, key_rows, value_rows = split_heads(pre_part, pre_pos, head_dim)
    pre_out = prefill_attention(queries, key_rows, value_rows, prior, offset)
    queries, key_rows, value_rows = split_heads(dec_part, dec_pos, head_dim)
    dec_out = decode_attention(queries, key_rows, value_rows, cache, lengths)
    columns = pre_out.shape[1] * pre_out.shape[2] * pre_out.shape[3]
    pre_out = pre_out.reshape(part_count, pre_rows, columns)
    dec_out = dec_out.reshape(part_count, -1, columns)
    return jnp.concatenate([pre_out, dec_out], axis=1).reshape(-1, columns)


def local(
    pre_tokens,
    dec_tokens,
    deal_slots,
    dec_lengths,
    pre_offsets,
    dec_cache,
    prior_cache,
    attn_gain,
    moe_gain,
    qkv_weight,
    out_weight,
    gate_up,
    down_weight,
    routes,
    route_gates,
):
    dp = ("zh", "dl")
    halves = lax.axis_size("zh")
    half_size = lax.axis_size("dl")
    group_count = halves * half_size
    part_count = lax.axis_size("mp")
    group_index = lax.axis_index("zh") * half_size + lax.axis_index("dl")
    part_index = lax.axis_index("mp")
    pre_rows = pre_tokens.shape[0]
    width = pre_tokens.shape[1]
    dec_rows = dec_tokens.shape[0]
    head_dim = dec_cache.shape[-1] // 2
    bundle = max(1, dec_rows // group_count)
    device = group_index * part_count + part_index
    position = jnp.arange(dec_rows, dtype=jnp.int32)
    own_deal = lax.dynamic_slice_in_dim(deal_slots, device * dec_rows, dec_rows, 0)
    target = own_deal // (part_count * dec_rows)
    group_ids = jnp.arange(group_count, dtype=jnp.int32)
    lane_ids = jnp.arange(bundle, dtype=jnp.int32)
    send_table = (
        (target[None, None, :] == group_ids[:, None, None])
        & (position[None, None, :] % bundle == lane_ids[None, :, None])
    ).astype(jnp.bfloat16)
    outgoing = jnp.einsum(
        "jbi,id->jbd", send_table, dec_tokens, preferred_element_type=jnp.float32
    ).astype(jnp.bfloat16)
    incoming = lax.all_to_all(outgoing, dp, split_axis=0, concat_axis=0, tiled=True)
    slot_ids = device * dec_rows + position
    request_ids = jnp.arange(deal_slots.shape[0], dtype=jnp.int32)
    request = jnp.sum(
        jnp.where(deal_slots[None, :] == slot_ids[:, None], request_ids[None, :], 0), axis=1
    )
    source = request // (part_count * dec_rows)
    lane = request % dec_rows % bundle
    take_table = (
        (source[:, None, None] == group_ids[None, :, None])
        & (lane[:, None, None] == lane_ids[None, None, :])
    ).astype(jnp.bfloat16)
    slot_rows = jnp.einsum(
        "ijb,jbd->id", take_table, incoming, preferred_element_type=jnp.float32
    ).astype(jnp.bfloat16)
    layer_input = jnp.concatenate([pre_tokens, slot_rows], axis=0)
    rows_dev = layer_input.shape[0]
    normed = root_norm(layer_input.astype(jnp.float32), attn_gain).astype(jnp.bfloat16)
    group_rows = lax.all_gather(normed, "mp", axis=0, tiled=True)
    local_width = qkv_weight.shape[1]
    qkv_pair = lax.all_gather(qkv_weight, "zh", axis=0, tiled=False)
    qkv_full = lax.all_gather(qkv_pair, "dl", axis=0, tiled=False)
    qkv_full = jnp.swapaxes(qkv_full, 0, 1).reshape(-1, local_width)
    projected = jnp.dot(group_rows, qkv_full, preferred_element_type=jnp.float32)
    local_groups = dec_cache.shape[0]
    projected = projected.reshape(part_count, rows_dev, local_groups, local_width // local_groups)
    attn_out = group_attention(
        projected, prior_cache[:, 0], dec_cache, dec_lengths, pre_offsets[0], pre_rows, head_dim
    )
    out_pair = lax.all_gather(out_weight, "zh", axis=1, tiled=False)
    out_full = lax.all_gather(out_pair, "dl", axis=1, tiled=False)
    out_full = jnp.swapaxes(out_full, 1, 2).reshape(out_weight.shape[0], -1)
    partial_sums = jnp.dot(attn_out, out_full, preferred_element_type=jnp.float32)
    attn_sum = lax.psum_scatter(
        partial_sums.astype(jnp.bfloat16), "mp", scatter_dimension=0, tiled=True
    ).astype(jnp.float32)
    residual = layer_input.astype(jnp.float32) + attn_sum
    normed_moe = root_norm(residual, moe_gain).astype(jnp.bfloat16)
    expert_count = gate_up.shape[0]
    local_experts = max(1, expert_count // half_size)
    copies = max(1, half_size // expert_count)

    def owner_major(weights):
        per_half = jnp.repeat(weights, copies, axis=0).reshape(
            (half_size, local_experts) + weights.shape[1:]
        )
        both = jnp.broadcast_to(per_half[None], (halves,) + per_half.shape)
        return both.reshape((group_count, local_experts) + weights.shape[1:])

    owned_gu, owned_dn = (
        lax.all_to_all(owner_major(gate_up), dp, split_axis=0, concat_axis=2, tiled=True),
        lax.all_to_all(owner_major(down_weight), dp, split_axis=0, concat_axis=2, tiled=True),
    )
    full_gu, full_dn = (
        lax.all_gather(owned_gu, "mp", axis=3, tiled=True),
        lax.all_gather(owned_dn, "mp", axis=3, tiled=True),
    )
    full_gu = full_gu[0]
    full_dn = full_dn[0]
    topk = routes.shape[1]
    capacity = 4 * ((rows_dev * topk + 3 * expert_count - 1) // (3 * expert_count))
    expert_ids = jnp.arange(expert_count, dtype=jnp.int32)
    hits = routes[:, :, None] == expert_ids[None, None, :]
    chosen = jnp.any(hits, axis=1)
    weight = jnp.sum(jnp.where(hits, route_gates.astype(jnp.float32)[:, :, None], 0.0), axis=1)
    rank = jnp.cumsum(chosen.astype(jnp.int32), axis=0) - 1
    slot_range = jnp.arange(capacity, dtype=jnp.int32)
    placed = chosen.T[:, None, :] & (rank.T[:, None, :] == slot_range[None, :, None])
    dispatch_table = placed.astype(jnp.bfloat16)
    outbound = jnp.einsum(
        "ecr,rd->ecd", dispatch_table, normed_moe, preferred_element_type=jnp.float32
    ).astype(jnp.bfloat16)
    per_owner = expert_count * capacity // half_size
    outbound = outbound.reshape(half_size, local_experts, per_owner // local_experts, width)
    both = jnp.einsum(
        "slnd,ldf->slnf",
        lax.all_to_all(outbound, "dl", split_axis=0, concat_axis=0, tiled=True),
        full_gu,
        preferred_element_type=jnp.float32,
    )
    halfway = both.shape[-1] // 2
    activation = (jax.nn.silu(both[..., :halfway]) * both[..., halfway:]).astype(jnp.bfloat16)
    expert_out = jnp.einsum(
        "slnf,lfd->slnd", activation, full_dn, preferred_element_type=jnp.float32
    ).astype(jnp.bfloat16)
    returned = lax.all_to_all(expert_out, "dl", split_axis=0, concat_axis=0, tiled=True)
    returned = returned.reshape(expert_count, capacity, width)
    combine_table = (placed.astype(jnp.float32) * weight.T[:, None, :]).astype(jnp.bfloat16)
    moe_sum = jnp.einsum("ecr,ecd->rd", combine_table, returned, preferred_element_type=jnp.float32)
    return (residual + moe_sum).astype(jnp.bfloat16)


def solution(mesh):
    groups = mesh.shape["dp"]
    halves = 2 if groups % 2 == 0 else 1
    devices = mesh.devices.reshape(halves, groups // halves, mesh.shape["mp"])
    split_mesh = jax.sharding.Mesh(devices, ("zh", "dl", "mp"))
    dp = ("zh", "dl")
    return jax.shard_map(
        local,
        mesh=split_mesh,
        in_specs=(
            P((*dp, "mp"), None),
            P((*dp, "mp"), None),
            P(),
            P(dp),
            P(dp),
            P("mp", dp, None, None),
            P("mp", dp, None, None),
            P(),
            P(),
            P(dp, "mp"),
            P("mp", dp),
            P(None, dp, "mp"),
            P(None, dp, "mp"),
            P((*dp, "mp"), None),
            P((*dp, "mp"), None),
        ),
        out_specs=P((*dp, "mp"), None),
        check_vma=False,
    )
```

```python
import jax
import jax.numpy as jnp
from jax import lax
from jax.sharding import PartitionSpec as P

EPSILON = 1e-06
ROTARY_BASE = 10000.0
SCORE_SCALE = 0.015625


def root_norm(values, gain):
    mean_square = jnp.mean(values * values, axis=-1, keepdims=True)
    return values * lax.rsqrt(mean_square + EPSILON) * gain


def rotary(vectors, positions):
    halfway = vectors.shape[-1] // 2
    freq_table = ROTARY_BASE ** (-jnp.arange(halfway).astype(jnp.float32) / halfway)
    angles = positions[..., None] * freq_table
    cosine = jnp.cos(angles)
    sine_part = jnp.sin(angles)
    leading = vectors[..., :halfway]
    trailing = vectors[..., halfway:]
    return jnp.concatenate(
        [leading * cosine - trailing * sine_part, trailing * cosine + leading * sine_part], axis=-1
    )


def split_heads(projected, positions, head_dim):
    per_group = projected.shape[-1] // head_dim - 2
    row_count = projected.shape[0]
    group_count = projected.shape[1]
    queries = projected[..., : per_group * head_dim].reshape(
        row_count, group_count, per_group, head_dim
    )
    key_rows = projected[..., per_group * head_dim : (per_group + 1) * head_dim]
    value_rows = projected[..., (per_group + 1) * head_dim :]
    queries = rotary(queries, positions[:, None, None]).astype(jnp.bfloat16)
    key_rows = rotary(key_rows, positions[:, None]).astype(jnp.bfloat16)
    return (queries, key_rows, value_rows.astype(jnp.bfloat16))


def prefill_attention(queries, key_rows, value_rows, prior, offset):
    head_dim = queries.shape[-1]
    row_count = queries.shape[0]
    span = prior.shape[1]
    all_keys = jnp.concatenate([prior[:, :, :head_dim], jnp.swapaxes(key_rows, 0, 1)], axis=1)
    all_values = jnp.concatenate([prior[:, :, head_dim:], jnp.swapaxes(value_rows, 0, 1)], axis=1)
    scores = (
        jnp.einsum("cgph,gkh->gpck", queries, all_keys, preferred_element_type=jnp.float32)
        * SCORE_SCALE
    )
    column = jnp.arange(span + row_count)
    row_ids = jnp.arange(row_count)
    allowed = jnp.where(
        column[None, :] < span, column[None, :] < offset, column[None, :] - span <= row_ids[:, None]
    )
    scores = jnp.where(allowed, scores, -jnp.inf)
    highest = jnp.max(scores, axis=-1, keepdims=True)
    expo = jnp.exp(scores - highest)
    weights = (expo / jnp.sum(expo, axis=-1, keepdims=True)).astype(jnp.bfloat16)
    mixed = jnp.einsum("gpck,gkh->cgph", weights, all_values, preferred_element_type=jnp.float32)
    return mixed.astype(jnp.bfloat16)


def decode_attention(queries, key_rows, value_rows, cache, lengths):
    head_dim = queries.shape[-1]
    cached = (
        jnp.einsum(
            "sgph,gslh->sgpl", queries, cache[..., :head_dim], preferred_element_type=jnp.float32
        )
        * SCORE_SCALE
    )
    own_score = (
        jnp.einsum("sgph,sgh->sgp", queries, key_rows, preferred_element_type=jnp.float32)
        * SCORE_SCALE
    )
    valid = jnp.arange(cache.shape[2])[None, :] < lengths[:, None]
    cached = jnp.where(valid[:, None, None, :], cached, -jnp.inf)
    highest = jnp.maximum(jnp.max(cached, axis=-1), own_score)
    expo = jnp.exp(cached - highest[..., None])
    own_expo = jnp.exp(own_score - highest)
    total = jnp.sum(expo, axis=-1) + own_expo
    weights = (expo / total[..., None]).astype(jnp.bfloat16)
    own_weight = (own_expo / total).astype(jnp.bfloat16)
    mixed = jnp.einsum(
        "sgpl,gslh->sgph", weights, cache[..., head_dim:], preferred_element_type=jnp.float32
    )
    mixed = (
        mixed
        + own_weight.astype(jnp.float32)[..., None] * value_rows.astype(jnp.float32)[:, :, None, :]
    )
    return mixed.astype(jnp.bfloat16)


def group_attention(projected, prior, cache, lengths, offset, pre_rows, head_dim):
    part_count = projected.shape[0]
    pre_part = projected[:, :pre_rows].reshape((-1,) + projected.shape[2:])
    dec_part = projected[:, pre_rows:].reshape((-1,) + projected.shape[2:])
    pre_pos = (offset + jnp.arange(pre_part.shape[0], dtype=jnp.int32)).astype(jnp.float32)
    dec_pos = lengths.astype(jnp.float32)
    queries, key_rows, value_rows = split_heads(pre_part, pre_pos, head_dim)
    pre_out = prefill_attention(queries, key_rows, value_rows, prior, offset)
    queries, key_rows, value_rows = split_heads(dec_part, dec_pos, head_dim)
    dec_out = decode_attention(queries, key_rows, value_rows, cache, lengths)
    columns = pre_out.shape[1] * pre_out.shape[2] * pre_out.shape[3]
    pre_out = pre_out.reshape(part_count, pre_rows, columns)
    dec_out = dec_out.reshape(part_count, -1, columns)
    return jnp.concatenate([pre_out, dec_out], axis=1).reshape(-1, columns)


def local(
    pre_tokens,
    dec_tokens,
    deal_slots,
    dec_lengths,
    pre_offsets,
    dec_cache,
    prior_cache,
    attn_gain,
    moe_gain,
    qkv_weight,
    out_weight,
    gate_up,
    down_weight,
    routes,
    route_gates,
):
    dp = ("zh", "dl")
    halves = lax.axis_size("zh")
    half_size = lax.axis_size("dl")
    group_count = halves * half_size
    part_count = lax.axis_size("mp")
    group_index = lax.axis_index("zh") * half_size + lax.axis_index("dl")
    part_index = lax.axis_index("mp")
    pre_rows = pre_tokens.shape[0]
    width = pre_tokens.shape[1]
    dec_rows = dec_tokens.shape[0]
    head_dim = dec_cache.shape[-1] // 2
    bundle = max(1, dec_rows // group_count)
    device = group_index * part_count + part_index
    position = jnp.arange(dec_rows, dtype=jnp.int32)
    own_deal = lax.dynamic_slice_in_dim(deal_slots, device * dec_rows, dec_rows, 0)
    target = own_deal // (part_count * dec_rows)
    group_ids = jnp.arange(group_count, dtype=jnp.int32)
    lane_ids = jnp.arange(bundle, dtype=jnp.int32)
    send_table = (
        (target[None, None, :] == group_ids[:, None, None])
        & (position[None, None, :] % bundle == lane_ids[None, :, None])
    ).astype(jnp.bfloat16)
    outgoing = jnp.einsum(
        "jbi,id->jbd", send_table, dec_tokens, preferred_element_type=jnp.float32
    ).astype(jnp.bfloat16)
    incoming = lax.all_to_all(outgoing, dp, split_axis=0, concat_axis=0, tiled=True)
    slot_ids = device * dec_rows + position
    request_ids = jnp.arange(deal_slots.shape[0], dtype=jnp.int32)
    request = jnp.sum(
        jnp.where(deal_slots[None, :] == slot_ids[:, None], request_ids[None, :], 0), axis=1
    )
    source = request // (part_count * dec_rows)
    lane = request % dec_rows % bundle
    take_table = (
        (source[:, None, None] == group_ids[None, :, None])
        & (lane[:, None, None] == lane_ids[None, None, :])
    ).astype(jnp.bfloat16)
    slot_rows = jnp.einsum(
        "ijb,jbd->id", take_table, incoming, preferred_element_type=jnp.float32
    ).astype(jnp.bfloat16)
    layer_input = jnp.concatenate([pre_tokens, slot_rows], axis=0)
    rows_dev = layer_input.shape[0]
    normed = root_norm(layer_input.astype(jnp.float32), attn_gain).astype(jnp.bfloat16)
    group_rows = lax.all_gather(normed, "mp", axis=0, tiled=True)
    local_width = qkv_weight.shape[1]
    qkv_pair = lax.all_gather(qkv_weight, "zh", axis=0, tiled=False)
    qkv_full = lax.all_gather(qkv_pair, "dl", axis=0, tiled=False)
    qkv_full = jnp.swapaxes(qkv_full, 0, 1).reshape(-1, local_width)
    projected = jnp.dot(group_rows, qkv_full, preferred_element_type=jnp.float32)
    local_groups = dec_cache.shape[0]
    projected = projected.reshape(part_count, rows_dev, local_groups, local_width // local_groups)
    attn_out = group_attention(
        projected, prior_cache[:, 0], dec_cache, dec_lengths, pre_offsets[0], pre_rows, head_dim
    )
    out_pair = lax.all_gather(out_weight, "zh", axis=1, tiled=False)
    out_full = lax.all_gather(out_pair, "dl", axis=1, tiled=False)
    out_full = jnp.swapaxes(out_full, 1, 2).reshape(out_weight.shape[0], -1)
    partial_sums = jnp.dot(attn_out, out_full, preferred_element_type=jnp.float32)
    attn_sum = lax.psum_scatter(
        partial_sums.astype(jnp.bfloat16), "mp", scatter_dimension=0, tiled=True
    ).astype(jnp.float32)
    residual = layer_input.astype(jnp.float32) + attn_sum
    normed_moe = root_norm(residual, moe_gain).astype(jnp.bfloat16)
    expert_count = gate_up.shape[0]
    local_experts = max(1, expert_count // half_size)
    copies = max(1, half_size // expert_count)

    def owner_major(weights):
        per_half = jnp.repeat(weights, copies, axis=0).reshape(
            (half_size, local_experts) + weights.shape[1:]
        )
        both = jnp.broadcast_to(per_half[None], (halves,) + per_half.shape)
        return both.reshape((group_count, local_experts) + weights.shape[1:])

    owned_gu, owned_dn = (
        lax.all_to_all(owner_major(gate_up), dp, split_axis=0, concat_axis=2, tiled=True),
        lax.all_to_all(owner_major(down_weight), dp, split_axis=0, concat_axis=2, tiled=True),
    )
    full_gu, full_dn = (
        lax.all_gather(owned_gu, "mp", axis=3, tiled=True),
        lax.all_gather(owned_dn, "mp", axis=3, tiled=True),
    )
    full_gu = full_gu[0]
    full_dn = full_dn[0]
    topk = routes.shape[1]
    capacity = 4 * ((rows_dev * topk + 3 * expert_count - 1) // (3 * expert_count))
    expert_ids = jnp.arange(expert_count, dtype=jnp.int32)
    hits = routes[:, :, None] == expert_ids[None, None, :]
    chosen = jnp.any(hits, axis=1)
    weight = jnp.sum(jnp.where(hits, route_gates.astype(jnp.float32)[:, :, None], 0.0), axis=1)
    rank = jnp.cumsum(chosen.astype(jnp.int32), axis=0) - 1
    slot_range = jnp.arange(capacity, dtype=jnp.int32)
    placed = chosen.T[:, None, :] & (rank.T[:, None, :] == slot_range[None, :, None])
    combine_table = (placed.astype(jnp.float32) * weight.T[:, None, :]).astype(jnp.bfloat16)
    halfway = full_gu.shape[-1] // 2
    if copies > 1:
        chunks = [(slice(None), 0)]
    else:
        chunks = [(slice(l, None, local_experts), l) for l in range(local_experts)]
    moe_sum = jnp.zeros((rows_dev, width), jnp.float32)
    for picked, l in chunks:
        table = placed[picked].astype(jnp.bfloat16)
        outbound = jnp.einsum(
            "ecr,rd->ecd", table, normed_moe, preferred_element_type=jnp.float32
        ).astype(jnp.bfloat16)
        outbound = outbound.reshape(half_size, -1, width)
        arrived = lax.all_to_all(outbound, "dl", split_axis=0, concat_axis=0, tiled=True)
        both = jnp.einsum(
            "snd,df->snf", arrived, full_gu[l], preferred_element_type=jnp.float32
        )
        activation = (jax.nn.silu(both[..., :halfway]) * both[..., halfway:]).astype(jnp.bfloat16)
        expert_out = jnp.einsum(
            "snf,fd->snd", activation, full_dn[l], preferred_element_type=jnp.float32
        ).astype(jnp.bfloat16)
        returned = lax.all_to_all(expert_out, "dl", split_axis=0, concat_axis=0, tiled=True)
        returned = returned.reshape(-1, capacity, width)
        moe_sum = moe_sum + jnp.einsum(
            "ecr,ecd->rd", combine_table[picked], returned, preferred_element_type=jnp.float32
        )
    return (residual + moe_sum).astype(jnp.bfloat16)


def solution(mesh):
    groups = mesh.shape["dp"]
    halves = 2 if groups % 2 == 0 else 1
    devices = mesh.devices.reshape(halves, groups // halves, mesh.shape["mp"])
    split_mesh = jax.sharding.Mesh(devices, ("zh", "dl", "mp"))
    dp = ("zh", "dl")
    return jax.shard_map(
        local,
        mesh=split_mesh,
        in_specs=(
            P((*dp, "mp"), None),
            P((*dp, "mp"), None),
            P(),
            P(dp),
            P(dp),
            P("mp", dp, None, None),
            P("mp", dp, None, None),
            P(),
            P(),
            P(dp, "mp"),
            P("mp", dp),
            P(None, dp, "mp"),
            P(None, dp, "mp"),
            P((*dp, "mp"), None),
            P((*dp, "mp"), None),
        ),
        out_specs=P((*dp, "mp"), None),
        check_vma=False,
    )
```

```python
import jax
import jax.numpy as jnp
from jax import lax
from jax.sharding import PartitionSpec as P

EPSILON = 1e-06
ROTARY_BASE = 10000.0
SCORE_SCALE = 0.015625


def root_norm(values, gain):
    mean_square = jnp.mean(values * values, axis=-1, keepdims=True)
    return values * lax.rsqrt(mean_square + EPSILON) * gain


def rotary(vectors, positions):
    halfway = vectors.shape[-1] // 2
    freq_table = ROTARY_BASE ** (-jnp.arange(halfway).astype(jnp.float32) / halfway)
    angles = positions[..., None] * freq_table
    cosine = jnp.cos(angles)
    sine_part = jnp.sin(angles)
    leading = vectors[..., :halfway]
    trailing = vectors[..., halfway:]
    return jnp.concatenate(
        [leading * cosine - trailing * sine_part, trailing * cosine + leading * sine_part], axis=-1
    )


def split_heads(projected, positions, head_dim):
    per_group = projected.shape[-1] // head_dim - 2
    row_count = projected.shape[0]
    group_count = projected.shape[1]
    queries = projected[..., : per_group * head_dim].reshape(
        row_count, group_count, per_group, head_dim
    )
    key_rows = projected[..., per_group * head_dim : (per_group + 1) * head_dim]
    value_rows = projected[..., (per_group + 1) * head_dim :]
    queries = rotary(queries, positions[:, None, None]).astype(jnp.bfloat16)
    key_rows = rotary(key_rows, positions[:, None]).astype(jnp.bfloat16)
    return (queries, key_rows, value_rows.astype(jnp.bfloat16))


def prefill_attention(queries, key_rows, value_rows, prior, offset):
    head_dim = queries.shape[-1]
    row_count = queries.shape[0]
    span = prior.shape[1]
    all_keys = jnp.concatenate([prior[:, :, :head_dim], jnp.swapaxes(key_rows, 0, 1)], axis=1)
    all_values = jnp.concatenate([prior[:, :, head_dim:], jnp.swapaxes(value_rows, 0, 1)], axis=1)
    scores = (
        jnp.einsum("cgph,gkh->gpck", queries, all_keys, preferred_element_type=jnp.float32)
        * SCORE_SCALE
    )
    column = jnp.arange(span + row_count)
    row_ids = jnp.arange(row_count)
    allowed = jnp.where(
        column[None, :] < span, column[None, :] < offset, column[None, :] - span <= row_ids[:, None]
    )
    scores = jnp.where(allowed, scores, -jnp.inf)
    highest = jnp.max(scores, axis=-1, keepdims=True)
    expo = jnp.exp(scores - highest)
    weights = (expo / jnp.sum(expo, axis=-1, keepdims=True)).astype(jnp.bfloat16)
    mixed = jnp.einsum("gpck,gkh->cgph", weights, all_values, preferred_element_type=jnp.float32)
    return mixed.astype(jnp.bfloat16)


def decode_attention(queries, key_rows, value_rows, cache, lengths):
    head_dim = queries.shape[-1]
    cached = (
        jnp.einsum(
            "sgph,gslh->sgpl", queries, cache[..., :head_dim], preferred_element_type=jnp.float32
        )
        * SCORE_SCALE
    )
    own_score = (
        jnp.einsum("sgph,sgh->sgp", queries, key_rows, preferred_element_type=jnp.float32)
        * SCORE_SCALE
    )
    valid = jnp.arange(cache.shape[2])[None, :] < lengths[:, None]
    cached = jnp.where(valid[:, None, None, :], cached, -jnp.inf)
    highest = jnp.maximum(jnp.max(cached, axis=-1), own_score)
    expo = jnp.exp(cached - highest[..., None])
    own_expo = jnp.exp(own_score - highest)
    total = jnp.sum(expo, axis=-1) + own_expo
    weights = (expo / total[..., None]).astype(jnp.bfloat16)
    own_weight = (own_expo / total).astype(jnp.bfloat16)
    mixed = jnp.einsum(
        "sgpl,gslh->sgph", weights, cache[..., head_dim:], preferred_element_type=jnp.float32
    )
    mixed = (
        mixed
        + own_weight.astype(jnp.float32)[..., None] * value_rows.astype(jnp.float32)[:, :, None, :]
    )
    return mixed.astype(jnp.bfloat16)


def group_attention(projected, prior, cache, lengths, offset, pre_rows, head_dim):
    part_count = projected.shape[0]
    pre_part = projected[:, :pre_rows].reshape((-1,) + projected.shape[2:])
    dec_part = projected[:, pre_rows:].reshape((-1,) + projected.shape[2:])
    pre_pos = (offset + jnp.arange(pre_part.shape[0], dtype=jnp.int32)).astype(jnp.float32)
    dec_pos = lengths.astype(jnp.float32)
    queries, key_rows, value_rows = split_heads(pre_part, pre_pos, head_dim)
    pre_out = prefill_attention(queries, key_rows, value_rows, prior, offset)
    queries, key_rows, value_rows = split_heads(dec_part, dec_pos, head_dim)
    dec_out = decode_attention(queries, key_rows, value_rows, cache, lengths)
    columns = pre_out.shape[1] * pre_out.shape[2] * pre_out.shape[3]
    pre_out = pre_out.reshape(part_count, pre_rows, columns)
    dec_out = dec_out.reshape(part_count, -1, columns)
    return jnp.concatenate([pre_out, dec_out], axis=1).reshape(-1, columns)


def across_halves(shard):
    halves = lax.axis_size("zh")
    if halves == 1:
        return shard[None]
    other = lax.ppermute(shard, "zh", [(0, 1), (1, 0)])
    first = lax.axis_index("zh") == 0
    return jnp.stack([jnp.where(first, shard, other), jnp.where(first, other, shard)])


def local(
    pre_tokens,
    dec_tokens,
    deal_slots,
    dec_lengths,
    pre_offsets,
    dec_cache,
    prior_cache,
    attn_gain,
    moe_gain,
    qkv_weight,
    out_weight,
    gate_up,
    down_weight,
    routes,
    route_gates,
):
    dp = ("zh", "dl")
    halves = lax.axis_size("zh")
    half_size = lax.axis_size("dl")
    group_count = halves * half_size
    part_count = lax.axis_size("mp")
    group_index = lax.axis_index("zh") * half_size + lax.axis_index("dl")
    part_index = lax.axis_index("mp")
    pre_rows = pre_tokens.shape[0]
    width = pre_tokens.shape[1]
    dec_rows = dec_tokens.shape[0]
    head_dim = dec_cache.shape[-1] // 2
    bundle = max(1, dec_rows // group_count)
    device = group_index * part_count + part_index
    position = jnp.arange(dec_rows, dtype=jnp.int32)
    own_deal = lax.dynamic_slice_in_dim(deal_slots, device * dec_rows, dec_rows, 0)
    target = own_deal // (part_count * dec_rows)
    group_ids = jnp.arange(group_count, dtype=jnp.int32)
    lane_ids = jnp.arange(bundle, dtype=jnp.int32)
    send_table = (
        (target[None, None, :] == group_ids[:, None, None])
        & (position[None, None, :] % bundle == lane_ids[None, :, None])
    ).astype(jnp.bfloat16)
    outgoing = jnp.einsum(
        "jbi,id->jbd", send_table, dec_tokens, preferred_element_type=jnp.float32
    ).astype(jnp.bfloat16)
    incoming = lax.all_to_all(outgoing, dp, split_axis=0, concat_axis=0, tiled=True)
    slot_ids = device * dec_rows + position
    request_ids = jnp.arange(deal_slots.shape[0], dtype=jnp.int32)
    request = jnp.sum(
        jnp.where(deal_slots[None, :] == slot_ids[:, None], request_ids[None, :], 0), axis=1
    )
    source = request // (part_count * dec_rows)
    lane = request % dec_rows % bundle
    take_table = (
        (source[:, None, None] == group_ids[None, :, None])
        & (lane[:, None, None] == lane_ids[None, None, :])
    ).astype(jnp.bfloat16)
    slot_rows = jnp.einsum(
        "ijb,jbd->id", take_table, incoming, preferred_element_type=jnp.float32
    ).astype(jnp.bfloat16)
    layer_input = jnp.concatenate([pre_tokens, slot_rows], axis=0)
    rows_dev = layer_input.shape[0]
    normed = root_norm(layer_input.astype(jnp.float32), attn_gain).astype(jnp.bfloat16)
    group_rows = lax.all_gather(normed, "mp", axis=0, tiled=True)
    local_width = qkv_weight.shape[1]
    qkv_pair = across_halves(qkv_weight)
    qkv_full = lax.all_gather(qkv_pair, "dl", axis=0, tiled=False)
    qkv_full = jnp.swapaxes(qkv_full, 0, 1).reshape(-1, local_width)
    qkv_full, out_source = lax.optimization_barrier((qkv_full, out_weight))
    projected = jnp.dot(group_rows, qkv_full, preferred_element_type=jnp.float32)
    local_groups = dec_cache.shape[0]
    projected = projected.reshape(part_count, rows_dev, local_groups, local_width // local_groups)
    attn_out = group_attention(
        projected, prior_cache[:, 0], dec_cache, dec_lengths, pre_offsets[0], pre_rows, head_dim
    )
    out_pair = jnp.moveaxis(across_halves(out_source), 0, 1)
    out_full = lax.all_gather(out_pair, "dl", axis=1, tiled=False)
    out_full = jnp.swapaxes(out_full, 1, 2).reshape(out_weight.shape[0], -1)
    partial_sums = jnp.dot(attn_out, out_full, preferred_element_type=jnp.float32)
    attn_sum = lax.psum_scatter(
        partial_sums.astype(jnp.bfloat16), "mp", scatter_dimension=0, tiled=True
    ).astype(jnp.float32)
    residual = layer_input.astype(jnp.float32) + attn_sum
    normed_moe = root_norm(residual, moe_gain).astype(jnp.bfloat16)
    expert_count = gate_up.shape[0]
    local_experts = max(1, expert_count // half_size)
    copies = max(1, half_size // expert_count)

    def owner_major(weights):
        per_half = jnp.repeat(weights, copies, axis=0).reshape(
            (half_size, local_experts) + weights.shape[1:]
        )
        both = jnp.broadcast_to(per_half[None], (halves,) + per_half.shape)
        return both.reshape((group_count, local_experts) + weights.shape[1:])

    gu_rows = gate_up.shape[1]
    owned = lax.all_to_all(
        jnp.concatenate([owner_major(gate_up), owner_major(down_weight)], axis=2),
        dp, split_axis=0, concat_axis=0, tiled=True,
    )
    owned_gu = jnp.moveaxis(owned[:, :, :gu_rows], 0, 1).reshape(
        (1, local_experts, -1) + gate_up.shape[2:]
    )
    owned_dn = jnp.moveaxis(owned[:, :, gu_rows:], 0, 1).reshape(
        (1, local_experts, -1) + down_weight.shape[2:]
    )
    full_gu, full_dn = (
        lax.all_gather(owned_gu, "mp", axis=3, tiled=True),
        lax.all_gather(owned_dn, "mp", axis=3, tiled=True),
    )
    full_gu = full_gu[0]
    full_dn = full_dn[0]
    topk = routes.shape[1]
    capacity = 4 * ((rows_dev * topk + 3 * expert_count - 1) // (3 * expert_count))
    expert_ids = jnp.arange(expert_count, dtype=jnp.int32)
    hits = routes[:, :, None] == expert_ids[None, None, :]
    chosen = jnp.any(hits, axis=1)
    weight = jnp.sum(jnp.where(hits, route_gates.astype(jnp.float32)[:, :, None], 0.0), axis=1)
    rank = jnp.cumsum(chosen.astype(jnp.int32), axis=0) - 1
    slot_range = jnp.arange(capacity, dtype=jnp.int32)
    placed = chosen.T[:, None, :] & (rank.T[:, None, :] == slot_range[None, :, None])
    combine_table = (placed.astype(jnp.float32) * weight.T[:, None, :]).astype(jnp.bfloat16)
    halfway = full_gu.shape[-1] // 2
    if copies > 1:
        chunks = [(slice(None), 0)]
    else:
        chunks = [(slice(l, None, local_experts), l) for l in range(local_experts)]
    moe_sum = jnp.zeros((rows_dev, width), jnp.float32)
    for picked, l in chunks:
        table = placed[picked].astype(jnp.bfloat16)
        outbound = jnp.einsum(
            "ecr,rd->ecd", table, normed_moe, preferred_element_type=jnp.float32
        ).astype(jnp.bfloat16)
        outbound = outbound.reshape(half_size, -1, width)
        arrived = lax.all_to_all(outbound, "dl", split_axis=0, concat_axis=0, tiled=True)
        both = jnp.einsum(
            "snd,df->snf", arrived, full_gu[l], preferred_element_type=jnp.float32
        )
        activation = (jax.nn.silu(both[..., :halfway]) * both[..., halfway:]).astype(jnp.bfloat16)
        expert_out = jnp.einsum(
            "snf,fd->snd", activation, full_dn[l], preferred_element_type=jnp.float32
        ).astype(jnp.bfloat16)
        returned = lax.all_to_all(expert_out, "dl", split_axis=0, concat_axis=0, tiled=True)
        returned = returned.reshape(-1, capacity, width)
        moe_sum = moe_sum + jnp.einsum(
            "ecr,ecd->rd", combine_table[picked], returned, preferred_element_type=jnp.float32
        )
    return (residual + moe_sum).astype(jnp.bfloat16)


def solution(mesh):
    groups = mesh.shape["dp"]
    halves = 2 if groups % 2 == 0 else 1
    devices = mesh.devices.reshape(halves, groups // halves, mesh.shape["mp"])
    split_mesh = jax.sharding.Mesh(devices, ("zh", "dl", "mp"))
    dp = ("zh", "dl")
    return jax.shard_map(
        local,
        mesh=split_mesh,
        in_specs=(
            P((*dp, "mp"), None),
            P((*dp, "mp"), None),
            P(),
            P(dp),
            P(dp),
            P("mp", dp, None, None),
            P("mp", dp, None, None),
            P(),
            P(),
            P(dp, "mp"),
            P("mp", dp),
            P(None, dp, "mp"),
            P(None, dp, "mp"),
            P((*dp, "mp"), None),
            P((*dp, "mp"), None),
        ),
        out_specs=P((*dp, "mp"), None),
        check_vma=False,
    )
```

```python
import jax
import jax.numpy as jnp
from jax import lax
from jax.sharding import PartitionSpec as P

EPSILON = 1e-06
ROTARY_BASE = 10000.0
SCORE_SCALE = 0.015625


def root_norm(values, gain):
    mean_square = jnp.mean(values * values, axis=-1, keepdims=True)
    return values * lax.rsqrt(mean_square + EPSILON) * gain


def rotary(vectors, positions):
    halfway = vectors.shape[-1] // 2
    freq_table = ROTARY_BASE ** (-jnp.arange(halfway).astype(jnp.float32) / halfway)
    angles = positions[..., None] * freq_table
    cosine = jnp.cos(angles)
    sine_part = jnp.sin(angles)
    leading = vectors[..., :halfway]
    trailing = vectors[..., halfway:]
    return jnp.concatenate(
        [leading * cosine - trailing * sine_part, trailing * cosine + leading * sine_part], axis=-1
    )


def split_heads(projected, positions, head_dim):
    per_group = projected.shape[-1] // head_dim - 2
    row_count = projected.shape[0]
    group_count = projected.shape[1]
    queries = projected[..., : per_group * head_dim].reshape(
        row_count, group_count, per_group, head_dim
    )
    key_rows = projected[..., per_group * head_dim : (per_group + 1) * head_dim]
    value_rows = projected[..., (per_group + 1) * head_dim :]
    queries = rotary(queries, positions[:, None, None]).astype(jnp.bfloat16)
    key_rows = rotary(key_rows, positions[:, None]).astype(jnp.bfloat16)
    return (queries, key_rows, value_rows.astype(jnp.bfloat16))


def prefill_attention(queries, key_rows, value_rows, prior, offset):
    head_dim = queries.shape[-1]
    row_count = queries.shape[0]
    span = prior.shape[1]
    all_keys = jnp.concatenate([prior[:, :, :head_dim], jnp.swapaxes(key_rows, 0, 1)], axis=1)
    all_values = jnp.concatenate([prior[:, :, head_dim:], jnp.swapaxes(value_rows, 0, 1)], axis=1)
    scores = (
        jnp.einsum("cgph,gkh->gpck", queries, all_keys, preferred_element_type=jnp.float32)
        * SCORE_SCALE
    )
    column = jnp.arange(span + row_count)
    row_ids = jnp.arange(row_count)
    allowed = jnp.where(
        column[None, :] < span, column[None, :] < offset, column[None, :] - span <= row_ids[:, None]
    )
    scores = jnp.where(allowed, scores, -jnp.inf)
    highest = jnp.max(scores, axis=-1, keepdims=True)
    expo = jnp.exp(scores - highest)
    weights = (expo / jnp.sum(expo, axis=-1, keepdims=True)).astype(jnp.bfloat16)
    mixed = jnp.einsum("gpck,gkh->cgph", weights, all_values, preferred_element_type=jnp.float32)
    return mixed.astype(jnp.bfloat16)


def decode_attention(queries, key_rows, value_rows, cache, lengths):
    head_dim = queries.shape[-1]
    cached = (
        jnp.einsum(
            "sgph,gslh->sgpl", queries, cache[..., :head_dim], preferred_element_type=jnp.float32
        )
        * SCORE_SCALE
    )
    own_score = (
        jnp.einsum("sgph,sgh->sgp", queries, key_rows, preferred_element_type=jnp.float32)
        * SCORE_SCALE
    )
    valid = jnp.arange(cache.shape[2])[None, :] < lengths[:, None]
    cached = jnp.where(valid[:, None, None, :], cached, -jnp.inf)
    highest = jnp.maximum(jnp.max(cached, axis=-1), own_score)
    expo = jnp.exp(cached - highest[..., None])
    own_expo = jnp.exp(own_score - highest)
    total = jnp.sum(expo, axis=-1) + own_expo
    weights = (expo / total[..., None]).astype(jnp.bfloat16)
    own_weight = (own_expo / total).astype(jnp.bfloat16)
    mixed = jnp.einsum(
        "sgpl,gslh->sgph", weights, cache[..., head_dim:], preferred_element_type=jnp.float32
    )
    mixed = (
        mixed
        + own_weight.astype(jnp.float32)[..., None] * value_rows.astype(jnp.float32)[:, :, None, :]
    )
    return mixed.astype(jnp.bfloat16)


def group_attention(projected, prior, cache, lengths, offset, pre_rows, head_dim):
    part_count = projected.shape[0]
    pre_part = projected[:, :pre_rows].reshape((-1,) + projected.shape[2:])
    dec_part = projected[:, pre_rows:].reshape((-1,) + projected.shape[2:])
    pre_pos = (offset + jnp.arange(pre_part.shape[0], dtype=jnp.int32)).astype(jnp.float32)
    dec_pos = lengths.astype(jnp.float32)
    queries, key_rows, value_rows = split_heads(pre_part, pre_pos, head_dim)
    pre_out = prefill_attention(queries, key_rows, value_rows, prior, offset)
    queries, key_rows, value_rows = split_heads(dec_part, dec_pos, head_dim)
    dec_out = decode_attention(queries, key_rows, value_rows, cache, lengths)
    columns = pre_out.shape[1] * pre_out.shape[2] * pre_out.shape[3]
    pre_out = pre_out.reshape(part_count, pre_rows, columns)
    dec_out = dec_out.reshape(part_count, -1, columns)
    return jnp.concatenate([pre_out, dec_out], axis=1).reshape(-1, columns)


def across_halves(shard):
    halves = lax.axis_size("zh")
    if halves == 1:
        return shard[None]
    other = lax.ppermute(shard, "zh", [(0, 1), (1, 0)])
    first = lax.axis_index("zh") == 0
    return jnp.stack([jnp.where(first, shard, other), jnp.where(first, other, shard)])


def local(
    pre_tokens,
    dec_tokens,
    deal_slots,
    dec_lengths,
    pre_offsets,
    dec_cache,
    prior_cache,
    attn_gain,
    moe_gain,
    qkv_weight,
    out_weight,
    gate_up,
    down_weight,
    routes,
    route_gates,
):
    dp = ("zh", "dl")
    halves = lax.axis_size("zh")
    half_size = lax.axis_size("dl")
    group_count = halves * half_size
    part_count = lax.axis_size("mp")
    group_index = lax.axis_index("zh") * half_size + lax.axis_index("dl")
    part_index = lax.axis_index("mp")
    pre_rows = pre_tokens.shape[0]
    width = pre_tokens.shape[1]
    dec_rows = dec_tokens.shape[0]
    head_dim = dec_cache.shape[-1] // 2
    bundle = max(1, dec_rows // group_count)
    device = group_index * part_count + part_index
    position = jnp.arange(dec_rows, dtype=jnp.int32)
    own_deal = lax.dynamic_slice_in_dim(deal_slots, device * dec_rows, dec_rows, 0)
    target = own_deal // (part_count * dec_rows)
    group_ids = jnp.arange(group_count, dtype=jnp.int32)
    lane_ids = jnp.arange(bundle, dtype=jnp.int32)
    send_table = (
        (target[None, None, :] == group_ids[:, None, None])
        & (position[None, None, :] % bundle == lane_ids[None, :, None])
    ).astype(jnp.bfloat16)
    outgoing = jnp.einsum(
        "jbi,id->jbd", send_table, dec_tokens, preferred_element_type=jnp.float32
    ).astype(jnp.bfloat16)
    incoming = lax.all_to_all(outgoing, dp, split_axis=0, concat_axis=0, tiled=True)
    slot_ids = device * dec_rows + position
    request_ids = jnp.arange(deal_slots.shape[0], dtype=jnp.int32)
    request = jnp.sum(
        jnp.where(deal_slots[None, :] == slot_ids[:, None], request_ids[None, :], 0), axis=1
    )
    source = request // (part_count * dec_rows)
    lane = request % dec_rows % bundle
    take_table = (
        (source[:, None, None] == group_ids[None, :, None])
        & (lane[:, None, None] == lane_ids[None, None, :])
    ).astype(jnp.bfloat16)
    slot_rows = jnp.einsum(
        "ijb,jbd->id", take_table, incoming, preferred_element_type=jnp.float32
    ).astype(jnp.bfloat16)
    layer_input = jnp.concatenate([pre_tokens, slot_rows], axis=0)
    rows_dev = layer_input.shape[0]
    normed = root_norm(layer_input.astype(jnp.float32), attn_gain).astype(jnp.bfloat16)
    group_rows = lax.all_gather(normed, "mp", axis=0, tiled=True)
    local_width = qkv_weight.shape[1]
    qkv_pair = across_halves(qkv_weight)
    out_pair = jnp.moveaxis(across_halves(out_weight), 0, 1)
    qkv_full = lax.all_gather(qkv_pair, "dl", axis=0, tiled=False)
    qkv_full = jnp.swapaxes(qkv_full, 0, 1).reshape(-1, local_width)
    qkv_full, out_pair = lax.optimization_barrier((qkv_full, out_pair))
    projected = jnp.dot(group_rows, qkv_full, preferred_element_type=jnp.float32)
    local_groups = dec_cache.shape[0]
    projected = projected.reshape(part_count, rows_dev, local_groups, local_width // local_groups)
    attn_out = group_attention(
        projected, prior_cache[:, 0], dec_cache, dec_lengths, pre_offsets[0], pre_rows, head_dim
    )
    out_full = lax.all_gather(out_pair, "dl", axis=1, tiled=False)
    out_full = jnp.swapaxes(out_full, 1, 2).reshape(out_weight.shape[0], -1)
    partial_sums = jnp.dot(attn_out, out_full, preferred_element_type=jnp.float32)
    attn_sum = lax.psum_scatter(
        partial_sums.astype(jnp.bfloat16), "mp", scatter_dimension=0, tiled=True
    ).astype(jnp.float32)
    residual = layer_input.astype(jnp.float32) + attn_sum
    normed_moe = root_norm(residual, moe_gain).astype(jnp.bfloat16)
    expert_count = gate_up.shape[0]
    local_experts = max(1, expert_count // half_size)
    copies = max(1, half_size // expert_count)

    def owner_major(weights):
        per_half = jnp.repeat(weights, copies, axis=0).reshape(
            (half_size, local_experts) + weights.shape[1:]
        )
        both = jnp.broadcast_to(per_half[None], (halves,) + per_half.shape)
        return both.reshape((group_count, local_experts) + weights.shape[1:])

    gu_rows = gate_up.shape[1]
    owned = lax.all_to_all(
        jnp.concatenate([owner_major(gate_up), owner_major(down_weight)], axis=2),
        dp, split_axis=0, concat_axis=0, tiled=True,
    )
    owned_gu = jnp.moveaxis(owned[:, :, :gu_rows], 0, 1).reshape(
        (1, local_experts, -1) + gate_up.shape[2:]
    )
    owned_dn = jnp.moveaxis(owned[:, :, gu_rows:], 0, 1).reshape(
        (1, local_experts, -1) + down_weight.shape[2:]
    )
    full_gu, full_dn = (
        lax.all_gather(owned_gu, "mp", axis=3, tiled=True),
        lax.all_gather(owned_dn, "mp", axis=3, tiled=True),
    )
    full_gu = full_gu[0]
    full_dn = full_dn[0]
    topk = routes.shape[1]
    capacity = 4 * ((rows_dev * topk + 3 * expert_count - 1) // (3 * expert_count))
    expert_ids = jnp.arange(expert_count, dtype=jnp.int32)
    hits = routes[:, :, None] == expert_ids[None, None, :]
    chosen = jnp.any(hits, axis=1)
    weight = jnp.sum(jnp.where(hits, route_gates.astype(jnp.float32)[:, :, None], 0.0), axis=1)
    rank = jnp.cumsum(chosen.astype(jnp.int32), axis=0) - 1
    slot_range = jnp.arange(capacity, dtype=jnp.int32)
    placed = chosen.T[:, None, :] & (rank.T[:, None, :] == slot_range[None, :, None])
    combine_table = (placed.astype(jnp.float32) * weight.T[:, None, :]).astype(jnp.bfloat16)
    halfway = full_gu.shape[-1] // 2
    if copies > 1:
        chunks = [(slice(None), 0)]
    else:
        chunks = [(slice(l, None, local_experts), l) for l in range(local_experts)]
    moe_sum = jnp.zeros((rows_dev, width), jnp.float32)
    for picked, l in chunks:
        table = placed[picked].astype(jnp.bfloat16)
        outbound = jnp.einsum(
            "ecr,rd->ecd", table, normed_moe, preferred_element_type=jnp.float32
        ).astype(jnp.bfloat16)
        outbound = outbound.reshape(half_size, -1, width)
        arrived = lax.all_to_all(outbound, "dl", split_axis=0, concat_axis=0, tiled=True)
        both = jnp.einsum(
            "snd,df->snf", arrived, full_gu[l], preferred_element_type=jnp.float32
        )
        activation = (jax.nn.silu(both[..., :halfway]) * both[..., halfway:]).astype(jnp.bfloat16)
        expert_out = jnp.einsum(
            "snf,fd->snd", activation, full_dn[l], preferred_element_type=jnp.float32
        ).astype(jnp.bfloat16)
        returned = lax.all_to_all(expert_out, "dl", split_axis=0, concat_axis=0, tiled=True)
        returned = returned.reshape(-1, capacity, width)
        moe_sum = moe_sum + jnp.einsum(
            "ecr,ecd->rd", combine_table[picked], returned, preferred_element_type=jnp.float32
        )
    return (residual + moe_sum).astype(jnp.bfloat16)


def solution(mesh):
    groups = mesh.shape["dp"]
    halves = 2 if groups % 2 == 0 else 1
    devices = mesh.devices.reshape(halves, groups // halves, mesh.shape["mp"])
    split_mesh = jax.sharding.Mesh(devices, ("zh", "dl", "mp"))
    dp = ("zh", "dl")
    return jax.shard_map(
        local,
        mesh=split_mesh,
        in_specs=(
            P((*dp, "mp"), None),
            P((*dp, "mp"), None),
            P(),
            P(dp),
            P(dp),
            P("mp", dp, None, None),
            P("mp", dp, None, None),
            P(),
            P(),
            P(dp, "mp"),
            P("mp", dp),
            P(None, dp, "mp"),
            P(None, dp, "mp"),
            P((*dp, "mp"), None),
            P((*dp, "mp"), None),
        ),
        out_specs=P((*dp, "mp"), None),
        check_vma=False,
    )
```

```python
import jax
import jax.numpy as jnp
from jax import lax
from jax.sharding import PartitionSpec as P

EPSILON = 1e-06
ROTARY_BASE = 10000.0
SCORE_SCALE = 0.015625


def root_norm(values, gain):
    mean_square = jnp.mean(values * values, axis=-1, keepdims=True)
    return values * lax.rsqrt(mean_square + EPSILON) * gain


def rotary(vectors, positions):
    halfway = vectors.shape[-1] // 2
    freq_table = ROTARY_BASE ** (-jnp.arange(halfway).astype(jnp.float32) / halfway)
    angles = positions[..., None] * freq_table
    cosine = jnp.cos(angles)
    sine_part = jnp.sin(angles)
    leading = vectors[..., :halfway]
    trailing = vectors[..., halfway:]
    return jnp.concatenate(
        [leading * cosine - trailing * sine_part, trailing * cosine + leading * sine_part], axis=-1
    )


def split_heads(projected, positions, head_dim):
    per_group = projected.shape[-1] // head_dim - 2
    row_count = projected.shape[0]
    group_count = projected.shape[1]
    queries = projected[..., : per_group * head_dim].reshape(
        row_count, group_count, per_group, head_dim
    )
    key_rows = projected[..., per_group * head_dim : (per_group + 1) * head_dim]
    value_rows = projected[..., (per_group + 1) * head_dim :]
    queries = rotary(queries, positions[:, None, None]).astype(jnp.bfloat16)
    key_rows = rotary(key_rows, positions[:, None]).astype(jnp.bfloat16)
    return (queries, key_rows, value_rows.astype(jnp.bfloat16))


def prefill_attention(queries, key_rows, value_rows, prior, offset):
    head_dim = queries.shape[-1]
    row_count = queries.shape[0]
    span = prior.shape[1]
    all_keys = jnp.concatenate([prior[:, :, :head_dim], jnp.swapaxes(key_rows, 0, 1)], axis=1)
    all_values = jnp.concatenate([prior[:, :, head_dim:], jnp.swapaxes(value_rows, 0, 1)], axis=1)
    scores = (
        jnp.einsum("cgph,gkh->gpck", queries, all_keys, preferred_element_type=jnp.float32)
        * SCORE_SCALE
    )
    column = jnp.arange(span + row_count)
    row_ids = jnp.arange(row_count)
    allowed = jnp.where(
        column[None, :] < span, column[None, :] < offset, column[None, :] - span <= row_ids[:, None]
    )
    scores = jnp.where(allowed, scores, -jnp.inf)
    highest = jnp.max(scores, axis=-1, keepdims=True)
    expo = jnp.exp(scores - highest)
    weights = (expo / jnp.sum(expo, axis=-1, keepdims=True)).astype(jnp.bfloat16)
    mixed = jnp.einsum("gpck,gkh->cgph", weights, all_values, preferred_element_type=jnp.float32)
    return mixed.astype(jnp.bfloat16)


def decode_attention(queries, key_rows, value_rows, cache, lengths):
    head_dim = queries.shape[-1]
    cached = (
        jnp.einsum(
            "sgph,gslh->sgpl", queries, cache[..., :head_dim], preferred_element_type=jnp.float32
        )
        * SCORE_SCALE
    )
    own_score = (
        jnp.einsum("sgph,sgh->sgp", queries, key_rows, preferred_element_type=jnp.float32)
        * SCORE_SCALE
    )
    valid = jnp.arange(cache.shape[2])[None, :] < lengths[:, None]
    cached = jnp.where(valid[:, None, None, :], cached, -jnp.inf)
    highest = jnp.maximum(jnp.max(cached, axis=-1), own_score)
    expo = jnp.exp(cached - highest[..., None])
    own_expo = jnp.exp(own_score - highest)
    total = jnp.sum(expo, axis=-1) + own_expo
    weights = (expo / total[..., None]).astype(jnp.bfloat16)
    own_weight = (own_expo / total).astype(jnp.bfloat16)
    mixed = jnp.einsum(
        "sgpl,gslh->sgph", weights, cache[..., head_dim:], preferred_element_type=jnp.float32
    )
    mixed = (
        mixed
        + own_weight.astype(jnp.float32)[..., None] * value_rows.astype(jnp.float32)[:, :, None, :]
    )
    return mixed.astype(jnp.bfloat16)


def group_attention(projected, prior, cache, lengths, offset, pre_rows, head_dim):
    part_count = projected.shape[0]
    pre_part = projected[:, :pre_rows].reshape((-1,) + projected.shape[2:])
    dec_part = projected[:, pre_rows:].reshape((-1,) + projected.shape[2:])
    pre_pos = (offset + jnp.arange(pre_part.shape[0], dtype=jnp.int32)).astype(jnp.float32)
    dec_pos = lengths.astype(jnp.float32)
    queries, key_rows, value_rows = split_heads(pre_part, pre_pos, head_dim)
    pre_out = prefill_attention(queries, key_rows, value_rows, prior, offset)
    queries, key_rows, value_rows = split_heads(dec_part, dec_pos, head_dim)
    dec_out = decode_attention(queries, key_rows, value_rows, cache, lengths)
    columns = pre_out.shape[1] * pre_out.shape[2] * pre_out.shape[3]
    pre_out = pre_out.reshape(part_count, pre_rows, columns)
    dec_out = dec_out.reshape(part_count, -1, columns)
    return jnp.concatenate([pre_out, dec_out], axis=1).reshape(-1, columns)


def across_halves(shard):
    halves = lax.axis_size("zh")
    if halves == 1:
        return shard[None]
    other = lax.ppermute(shard, "zh", [(0, 1), (1, 0)])
    first = lax.axis_index("zh") == 0
    return jnp.stack([jnp.where(first, shard, other), jnp.where(first, other, shard)])


def local(
    pre_tokens,
    dec_tokens,
    deal_slots,
    dec_lengths,
    pre_offsets,
    dec_cache,
    prior_cache,
    attn_gain,
    moe_gain,
    qkv_weight,
    out_weight,
    gate_up,
    down_weight,
    routes,
    route_gates,
):
    dp = ("zh", "dl")
    halves = lax.axis_size("zh")
    half_size = lax.axis_size("dl")
    group_count = halves * half_size
    part_count = lax.axis_size("mp")
    group_index = lax.axis_index("zh") * half_size + lax.axis_index("dl")
    part_index = lax.axis_index("mp")
    pre_rows = pre_tokens.shape[0]
    width = pre_tokens.shape[1]
    dec_rows = dec_tokens.shape[0]
    head_dim = dec_cache.shape[-1] // 2
    bundle = max(1, dec_rows // group_count)
    device = group_index * part_count + part_index
    position = jnp.arange(dec_rows, dtype=jnp.int32)
    slot_ids = device * dec_rows + position
    request_ids = jnp.arange(deal_slots.shape[0], dtype=jnp.int32)
    take_table = (deal_slots[None, :] == slot_ids[:, None]).astype(jnp.bfloat16)
    local_width = qkv_weight.shape[1]
    qkv_pair = across_halves(qkv_weight)
    out_pair = jnp.moveaxis(across_halves(out_weight), 0, 1)
    qkv_full = lax.all_gather(qkv_pair, "dl", axis=0, tiled=False)
    qkv_full = jnp.swapaxes(qkv_full, 0, 1).reshape(-1, local_width)
    qkv_full, dec_tokens = lax.optimization_barrier((qkv_full, dec_tokens))
    every_request = lax.all_gather(dec_tokens, (*dp, "mp"), axis=0, tiled=True)
    every_request, out_pair = lax.optimization_barrier((every_request, out_pair))
    slot_rows = jnp.dot(
        take_table, every_request, preferred_element_type=jnp.float32
    ).astype(jnp.bfloat16)
    layer_input = jnp.concatenate([pre_tokens, slot_rows], axis=0)
    rows_dev = layer_input.shape[0]
    normed = root_norm(layer_input.astype(jnp.float32), attn_gain).astype(jnp.bfloat16)
    group_rows = lax.all_gather(normed, "mp", axis=0, tiled=True)
    projected = jnp.dot(group_rows, qkv_full, preferred_element_type=jnp.float32)
    local_groups = dec_cache.shape[0]
    projected = projected.reshape(part_count, rows_dev, local_groups, local_width // local_groups)
    attn_out = group_attention(
        projected, prior_cache[:, 0], dec_cache, dec_lengths, pre_offsets[0], pre_rows, head_dim
    )
    out_full = lax.all_gather(out_pair, "dl", axis=1, tiled=False)
    out_full = jnp.swapaxes(out_full, 1, 2).reshape(out_weight.shape[0], -1)
    partial_sums = jnp.dot(attn_out, out_full, preferred_element_type=jnp.float32)
    attn_sum = lax.psum_scatter(
        partial_sums.astype(jnp.bfloat16), "mp", scatter_dimension=0, tiled=True
    ).astype(jnp.float32)
    residual = layer_input.astype(jnp.float32) + attn_sum
    normed_moe = root_norm(residual, moe_gain).astype(jnp.bfloat16)
    expert_count = gate_up.shape[0]
    local_experts = max(1, expert_count // half_size)
    copies = max(1, half_size // expert_count)

    def owner_major(weights):
        per_half = jnp.repeat(weights, copies, axis=0).reshape(
            (half_size, local_experts) + weights.shape[1:]
        )
        both = jnp.broadcast_to(per_half[None], (halves,) + per_half.shape)
        return both.reshape((group_count, local_experts) + weights.shape[1:])

    gu_rows = gate_up.shape[1]
    owned = lax.all_to_all(
        jnp.concatenate([owner_major(gate_up), owner_major(down_weight)], axis=2),
        dp, split_axis=0, concat_axis=0, tiled=True,
    )
    owned_gu = jnp.moveaxis(owned[:, :, :gu_rows], 0, 1).reshape(
        (1, local_experts, -1) + gate_up.shape[2:]
    )
    owned_dn = jnp.moveaxis(owned[:, :, gu_rows:], 0, 1).reshape(
        (1, local_experts, -1) + down_weight.shape[2:]
    )
    full_gu, full_dn = (
        lax.all_gather(owned_gu, "mp", axis=3, tiled=True),
        lax.all_gather(owned_dn, "mp", axis=3, tiled=True),
    )
    full_gu = full_gu[0]
    full_dn = full_dn[0]
    topk = routes.shape[1]
    capacity = 4 * ((rows_dev * topk + 3 * expert_count - 1) // (3 * expert_count))
    expert_ids = jnp.arange(expert_count, dtype=jnp.int32)
    hits = routes[:, :, None] == expert_ids[None, None, :]
    chosen = jnp.any(hits, axis=1)
    weight = jnp.sum(jnp.where(hits, route_gates.astype(jnp.float32)[:, :, None], 0.0), axis=1)
    rank = jnp.cumsum(chosen.astype(jnp.int32), axis=0) - 1
    slot_range = jnp.arange(capacity, dtype=jnp.int32)
    placed = chosen.T[:, None, :] & (rank.T[:, None, :] == slot_range[None, :, None])
    combine_table = (placed.astype(jnp.float32) * weight.T[:, None, :]).astype(jnp.bfloat16)
    halfway = full_gu.shape[-1] // 2
    if copies > 1:
        chunks = [(slice(None), 0)]
    else:
        chunks = [(slice(l, None, local_experts), l) for l in range(local_experts)]
    moe_sum = jnp.zeros((rows_dev, width), jnp.float32)
    for picked, l in chunks:
        table = placed[picked].astype(jnp.bfloat16)
        outbound = jnp.einsum(
            "ecr,rd->ecd", table, normed_moe, preferred_element_type=jnp.float32
        ).astype(jnp.bfloat16)
        outbound = outbound.reshape(half_size, -1, width)
        arrived = lax.all_to_all(outbound, "dl", split_axis=0, concat_axis=0, tiled=True)
        both = jnp.einsum(
            "snd,df->snf", arrived, full_gu[l], preferred_element_type=jnp.float32
        )
        activation = (jax.nn.silu(both[..., :halfway]) * both[..., halfway:]).astype(jnp.bfloat16)
        expert_out = jnp.einsum(
            "snf,fd->snd", activation, full_dn[l], preferred_element_type=jnp.float32
        ).astype(jnp.bfloat16)
        returned = lax.all_to_all(expert_out, "dl", split_axis=0, concat_axis=0, tiled=True)
        returned = returned.reshape(-1, capacity, width)
        moe_sum = moe_sum + jnp.einsum(
            "ecr,ecd->rd", combine_table[picked], returned, preferred_element_type=jnp.float32
        )
    return (residual + moe_sum).astype(jnp.bfloat16)


def solution(mesh):
    groups = mesh.shape["dp"]
    halves = 2 if groups % 2 == 0 else 1
    devices = mesh.devices.reshape(halves, groups // halves, mesh.shape["mp"])
    split_mesh = jax.sharding.Mesh(devices, ("zh", "dl", "mp"))
    dp = ("zh", "dl")
    return jax.shard_map(
        local,
        mesh=split_mesh,
        in_specs=(
            P((*dp, "mp"), None),
            P((*dp, "mp"), None),
            P(),
            P(dp),
            P(dp),
            P("mp", dp, None, None),
            P("mp", dp, None, None),
            P(),
            P(),
            P(dp, "mp"),
            P("mp", dp),
            P(None, dp, "mp"),
            P(None, dp, "mp"),
            P((*dp, "mp"), None),
            P((*dp, "mp"), None),
        ),
        out_specs=P((*dp, "mp"), None),
        check_vma=False,
    )
```

```python
import jax
import jax.numpy as jnp
from jax import lax
from jax.sharding import PartitionSpec as P

EPSILON = 1e-06
ROTARY_BASE = 10000.0
SCORE_SCALE = 0.015625


def root_norm(values, gain):
    mean_square = jnp.mean(values * values, axis=-1, keepdims=True)
    return values * lax.rsqrt(mean_square + EPSILON) * gain


def rotary(vectors, positions):
    halfway = vectors.shape[-1] // 2
    freq_table = ROTARY_BASE ** (-jnp.arange(halfway).astype(jnp.float32) / halfway)
    angles = positions[..., None] * freq_table
    cosine = jnp.cos(angles)
    sine_part = jnp.sin(angles)
    leading = vectors[..., :halfway]
    trailing = vectors[..., halfway:]
    return jnp.concatenate(
        [leading * cosine - trailing * sine_part, trailing * cosine + leading * sine_part], axis=-1
    )


def split_heads(projected, positions, head_dim):
    per_group = projected.shape[-1] // head_dim - 2
    row_count = projected.shape[0]
    group_count = projected.shape[1]
    queries = projected[..., : per_group * head_dim].reshape(
        row_count, group_count, per_group, head_dim
    )
    key_rows = projected[..., per_group * head_dim : (per_group + 1) * head_dim]
    value_rows = projected[..., (per_group + 1) * head_dim :]
    queries = rotary(queries, positions[:, None, None]).astype(jnp.bfloat16)
    key_rows = rotary(key_rows, positions[:, None]).astype(jnp.bfloat16)
    return (queries, key_rows, value_rows.astype(jnp.bfloat16))


def prefill_attention(queries, key_rows, value_rows, prior, offset):
    head_dim = queries.shape[-1]
    row_count = queries.shape[0]
    span = prior.shape[1]
    all_keys = jnp.concatenate([prior[:, :, :head_dim], jnp.swapaxes(key_rows, 0, 1)], axis=1)
    all_values = jnp.concatenate([prior[:, :, head_dim:], jnp.swapaxes(value_rows, 0, 1)], axis=1)
    scores = (
        jnp.einsum("cgph,gkh->gpck", queries, all_keys, preferred_element_type=jnp.float32)
        * SCORE_SCALE
    )
    column = jnp.arange(span + row_count)
    row_ids = jnp.arange(row_count)
    allowed = jnp.where(
        column[None, :] < span, column[None, :] < offset, column[None, :] - span <= row_ids[:, None]
    )
    scores = jnp.where(allowed, scores, -jnp.inf)
    highest = jnp.max(scores, axis=-1, keepdims=True)
    expo = jnp.exp(scores - highest)
    weights = (expo / jnp.sum(expo, axis=-1, keepdims=True)).astype(jnp.bfloat16)
    mixed = jnp.einsum("gpck,gkh->cgph", weights, all_values, preferred_element_type=jnp.float32)
    return mixed.astype(jnp.bfloat16)


def decode_attention(queries, key_rows, value_rows, cache, lengths):
    head_dim = queries.shape[-1]
    cached = (
        jnp.einsum(
            "sgph,gslh->sgpl", queries, cache[..., :head_dim], preferred_element_type=jnp.float32
        )
        * SCORE_SCALE
    )
    own_score = (
        jnp.einsum("sgph,sgh->sgp", queries, key_rows, preferred_element_type=jnp.float32)
        * SCORE_SCALE
    )
    valid = jnp.arange(cache.shape[2])[None, :] < lengths[:, None]
    cached = jnp.where(valid[:, None, None, :], cached, -jnp.inf)
    highest = jnp.maximum(jnp.max(cached, axis=-1), own_score)
    expo = jnp.exp(cached - highest[..., None])
    own_expo = jnp.exp(own_score - highest)
    total = jnp.sum(expo, axis=-1) + own_expo
    weights = (expo / total[..., None]).astype(jnp.bfloat16)
    own_weight = (own_expo / total).astype(jnp.bfloat16)
    mixed = jnp.einsum(
        "sgpl,gslh->sgph", weights, cache[..., head_dim:], preferred_element_type=jnp.float32
    )
    mixed = (
        mixed
        + own_weight.astype(jnp.float32)[..., None] * value_rows.astype(jnp.float32)[:, :, None, :]
    )
    return mixed.astype(jnp.bfloat16)


def group_attention(projected, prior, cache, lengths, offset, pre_rows, head_dim):
    part_count = projected.shape[0]
    pre_part = projected[:, :pre_rows].reshape((-1,) + projected.shape[2:])
    dec_part = projected[:, pre_rows:].reshape((-1,) + projected.shape[2:])
    pre_pos = (offset + jnp.arange(pre_part.shape[0], dtype=jnp.int32)).astype(jnp.float32)
    dec_pos = lengths.astype(jnp.float32)
    queries, key_rows, value_rows = split_heads(pre_part, pre_pos, head_dim)
    pre_out = prefill_attention(queries, key_rows, value_rows, prior, offset)
    queries, key_rows, value_rows = split_heads(dec_part, dec_pos, head_dim)
    dec_out = decode_attention(queries, key_rows, value_rows, cache, lengths)
    columns = pre_out.shape[1] * pre_out.shape[2] * pre_out.shape[3]
    pre_out = pre_out.reshape(part_count, pre_rows, columns)
    dec_out = dec_out.reshape(part_count, -1, columns)
    return jnp.concatenate([pre_out, dec_out], axis=1).reshape(-1, columns)


def across_halves(shard):
    halves = lax.axis_size("zh")
    if halves == 1:
        return shard[None]
    other = lax.ppermute(shard, "zh", [(0, 1), (1, 0)])
    first = lax.axis_index("zh") == 0
    return jnp.stack([jnp.where(first, shard, other), jnp.where(first, other, shard)])


def local(
    pre_tokens,
    dec_tokens,
    deal_slots,
    dec_lengths,
    pre_offsets,
    dec_cache,
    prior_cache,
    attn_gain,
    moe_gain,
    qkv_weight,
    out_weight,
    gate_up,
    down_weight,
    routes,
    route_gates,
):
    dp = ("zh", "dl")
    halves = lax.axis_size("zh")
    half_size = lax.axis_size("dl")
    group_count = halves * half_size
    part_count = lax.axis_size("mp")
    group_index = lax.axis_index("zh") * half_size + lax.axis_index("dl")
    part_index = lax.axis_index("mp")
    pre_rows = pre_tokens.shape[0]
    width = pre_tokens.shape[1]
    dec_rows = dec_tokens.shape[0]
    head_dim = dec_cache.shape[-1] // 2
    bundle = max(1, dec_rows // group_count)
    device = group_index * part_count + part_index
    position = jnp.arange(dec_rows, dtype=jnp.int32)
    slot_ids = device * dec_rows + position
    request_ids = jnp.arange(deal_slots.shape[0], dtype=jnp.int32)
    take_table = (deal_slots[None, :] == slot_ids[:, None]).astype(jnp.bfloat16)
    local_width = qkv_weight.shape[1]
    weight_rows = qkv_weight.shape[0]
    riders = jnp.concatenate([qkv_weight, dec_tokens.reshape(-1, local_width)], axis=0)
    qkv_pair = across_halves(riders)
    out_pair = jnp.moveaxis(across_halves(out_weight), 0, 1)
    gathered = jnp.swapaxes(lax.all_gather(qkv_pair, "dl", axis=0, tiled=False), 0, 1)
    qkv_full = gathered[:, :, :weight_rows].reshape(-1, local_width)
    every_request = gathered[:, :, weight_rows:].reshape(group_count, dec_rows, width)
    every_request = lax.all_gather(every_request, "mp", axis=1, tiled=False)
    every_request = every_request.reshape(-1, width)
    qkv_full, out_pair = lax.optimization_barrier((qkv_full, out_pair))
    slot_rows = jnp.dot(
        take_table, every_request, preferred_element_type=jnp.float32
    ).astype(jnp.bfloat16)
    layer_input = jnp.concatenate([pre_tokens, slot_rows], axis=0)
    rows_dev = layer_input.shape[0]
    normed = root_norm(layer_input.astype(jnp.float32), attn_gain).astype(jnp.bfloat16)
    group_rows = lax.all_gather(normed, "mp", axis=0, tiled=True)
    projected = jnp.dot(group_rows, qkv_full, preferred_element_type=jnp.float32)
    local_groups = dec_cache.shape[0]
    projected = projected.reshape(part_count, rows_dev, local_groups, local_width // local_groups)
    attn_out = group_attention(
        projected, prior_cache[:, 0], dec_cache, dec_lengths, pre_offsets[0], pre_rows, head_dim
    )
    out_full = lax.all_gather(out_pair, "dl", axis=1, tiled=False)
    out_full = jnp.swapaxes(out_full, 1, 2).reshape(out_weight.shape[0], -1)
    partial_sums = jnp.dot(attn_out, out_full, preferred_element_type=jnp.float32)
    attn_sum = lax.psum_scatter(
        partial_sums.astype(jnp.bfloat16), "mp", scatter_dimension=0, tiled=True
    ).astype(jnp.float32)
    residual = layer_input.astype(jnp.float32) + attn_sum
    normed_moe = root_norm(residual, moe_gain).astype(jnp.bfloat16)
    expert_count = gate_up.shape[0]
    local_experts = max(1, expert_count // half_size)
    copies = max(1, half_size // expert_count)

    def owner_major(weights):
        per_half = jnp.repeat(weights, copies, axis=0).reshape(
            (half_size, local_experts) + weights.shape[1:]
        )
        both = jnp.broadcast_to(per_half[None], (halves,) + per_half.shape)
        return both.reshape((group_count, local_experts) + weights.shape[1:])

    gu_rows = gate_up.shape[1]
    owned = lax.all_to_all(
        jnp.concatenate([owner_major(gate_up), owner_major(down_weight)], axis=2),
        dp, split_axis=0, concat_axis=0, tiled=True,
    )
    owned_gu = jnp.moveaxis(owned[:, :, :gu_rows], 0, 1).reshape(
        (1, local_experts, -1) + gate_up.shape[2:]
    )
    owned_dn = jnp.moveaxis(owned[:, :, gu_rows:], 0, 1).reshape(
        (1, local_experts, -1) + down_weight.shape[2:]
    )
    full_gu, full_dn = (
        lax.all_gather(owned_gu, "mp", axis=3, tiled=True),
        lax.all_gather(owned_dn, "mp", axis=3, tiled=True),
    )
    full_gu = full_gu[0]
    full_dn = full_dn[0]
    topk = routes.shape[1]
    capacity = 4 * ((rows_dev * topk + 3 * expert_count - 1) // (3 * expert_count))
    expert_ids = jnp.arange(expert_count, dtype=jnp.int32)
    hits = routes[:, :, None] == expert_ids[None, None, :]
    chosen = jnp.any(hits, axis=1)
    weight = jnp.sum(jnp.where(hits, route_gates.astype(jnp.float32)[:, :, None], 0.0), axis=1)
    rank = jnp.cumsum(chosen.astype(jnp.int32), axis=0) - 1
    slot_range = jnp.arange(capacity, dtype=jnp.int32)
    placed = chosen.T[:, None, :] & (rank.T[:, None, :] == slot_range[None, :, None])
    combine_table = (placed.astype(jnp.float32) * weight.T[:, None, :]).astype(jnp.bfloat16)
    halfway = full_gu.shape[-1] // 2
    if copies > 1:
        chunks = [(slice(None), 0)]
    else:
        chunks = [(slice(l, None, local_experts), l) for l in range(local_experts)]
    moe_sum = jnp.zeros((rows_dev, width), jnp.float32)
    for picked, l in chunks:
        table = placed[picked].astype(jnp.bfloat16)
        outbound = jnp.einsum(
            "ecr,rd->ecd", table, normed_moe, preferred_element_type=jnp.float32
        ).astype(jnp.bfloat16)
        outbound = outbound.reshape(half_size, -1, width)
        arrived = lax.all_to_all(outbound, "dl", split_axis=0, concat_axis=0, tiled=True)
        both = jnp.einsum(
            "snd,df->snf", arrived, full_gu[l], preferred_element_type=jnp.float32
        )
        activation = (jax.nn.silu(both[..., :halfway]) * both[..., halfway:]).astype(jnp.bfloat16)
        expert_out = jnp.einsum(
            "snf,fd->snd", activation, full_dn[l], preferred_element_type=jnp.float32
        ).astype(jnp.bfloat16)
        returned = lax.all_to_all(expert_out, "dl", split_axis=0, concat_axis=0, tiled=True)
        returned = returned.reshape(-1, capacity, width)
        moe_sum = moe_sum + jnp.einsum(
            "ecr,ecd->rd", combine_table[picked], returned, preferred_element_type=jnp.float32
        )
    return (residual + moe_sum).astype(jnp.bfloat16)


def solution(mesh):
    groups = mesh.shape["dp"]
    halves = 2 if groups % 2 == 0 else 1
    devices = mesh.devices.reshape(halves, groups // halves, mesh.shape["mp"])
    split_mesh = jax.sharding.Mesh(devices, ("zh", "dl", "mp"))
    dp = ("zh", "dl")
    return jax.shard_map(
        local,
        mesh=split_mesh,
        in_specs=(
            P((*dp, "mp"), None),
            P((*dp, "mp"), None),
            P(),
            P(dp),
            P(dp),
            P("mp", dp, None, None),
            P("mp", dp, None, None),
            P(),
            P(),
            P(dp, "mp"),
            P("mp", dp),
            P(None, dp, "mp"),
            P(None, dp, "mp"),
            P((*dp, "mp"), None),
            P((*dp, "mp"), None),
        ),
        out_specs=P((*dp, "mp"), None),
        check_vma=False,
    )
```

```python
import jax
import jax.numpy as jnp
from jax import lax
from jax.sharding import PartitionSpec as P

EPSILON = 1e-06
ROTARY_BASE = 10000.0
SCORE_SCALE = 0.015625
DL = ("dc", "core")


def root_norm(values, gain):
    mean_square = jnp.mean(values * values, axis=-1, keepdims=True)
    return values * lax.rsqrt(mean_square + EPSILON) * gain


def rotary(vectors, positions):
    halfway = vectors.shape[-1] // 2
    freq_table = ROTARY_BASE ** (-jnp.arange(halfway).astype(jnp.float32) / halfway)
    angles = positions[..., None] * freq_table
    cosine = jnp.cos(angles)
    sine_part = jnp.sin(angles)
    leading = vectors[..., :halfway]
    trailing = vectors[..., halfway:]
    return jnp.concatenate(
        [leading * cosine - trailing * sine_part, trailing * cosine + leading * sine_part], axis=-1
    )


def split_heads(projected, positions, head_dim):
    per_group = projected.shape[-1] // head_dim - 2
    row_count = projected.shape[0]
    group_count = projected.shape[1]
    queries = projected[..., : per_group * head_dim].reshape(
        row_count, group_count, per_group, head_dim
    )
    key_rows = projected[..., per_group * head_dim : (per_group + 1) * head_dim]
    value_rows = projected[..., (per_group + 1) * head_dim :]
    queries = rotary(queries, positions[:, None, None]).astype(jnp.bfloat16)
    key_rows = rotary(key_rows, positions[:, None]).astype(jnp.bfloat16)
    return (queries, key_rows, value_rows.astype(jnp.bfloat16))


def prefill_attention(queries, key_rows, value_rows, prior, offset):
    head_dim = queries.shape[-1]
    row_count = queries.shape[0]
    span = prior.shape[1]
    all_keys = jnp.concatenate([prior[:, :, :head_dim], jnp.swapaxes(key_rows, 0, 1)], axis=1)
    all_values = jnp.concatenate([prior[:, :, head_dim:], jnp.swapaxes(value_rows, 0, 1)], axis=1)
    scores = (
        jnp.einsum("cgph,gkh->gpck", queries, all_keys, preferred_element_type=jnp.float32)
        * SCORE_SCALE
    )
    column = jnp.arange(span + row_count)
    row_ids = jnp.arange(row_count)
    allowed = jnp.where(
        column[None, :] < span, column[None, :] < offset, column[None, :] - span <= row_ids[:, None]
    )
    scores = jnp.where(allowed, scores, -jnp.inf)
    highest = jnp.max(scores, axis=-1, keepdims=True)
    expo = jnp.exp(scores - highest)
    weights = (expo / jnp.sum(expo, axis=-1, keepdims=True)).astype(jnp.bfloat16)
    mixed = jnp.einsum("gpck,gkh->cgph", weights, all_values, preferred_element_type=jnp.float32)
    return mixed.astype(jnp.bfloat16)


def decode_attention(queries, key_rows, value_rows, cache, lengths):
    head_dim = queries.shape[-1]
    cached = (
        jnp.einsum(
            "sgph,gslh->sgpl", queries, cache[..., :head_dim], preferred_element_type=jnp.float32
        )
        * SCORE_SCALE
    )
    own_score = (
        jnp.einsum("sgph,sgh->sgp", queries, key_rows, preferred_element_type=jnp.float32)
        * SCORE_SCALE
    )
    valid = jnp.arange(cache.shape[2])[None, :] < lengths[:, None]
    cached = jnp.where(valid[:, None, None, :], cached, -jnp.inf)
    highest = jnp.maximum(jnp.max(cached, axis=-1), own_score)
    expo = jnp.exp(cached - highest[..., None])
    own_expo = jnp.exp(own_score - highest)
    total = jnp.sum(expo, axis=-1) + own_expo
    weights = (expo / total[..., None]).astype(jnp.bfloat16)
    own_weight = (own_expo / total).astype(jnp.bfloat16)
    mixed = jnp.einsum(
        "sgpl,gslh->sgph", weights, cache[..., head_dim:], preferred_element_type=jnp.float32
    )
    mixed = (
        mixed
        + own_weight.astype(jnp.float32)[..., None] * value_rows.astype(jnp.float32)[:, :, None, :]
    )
    return mixed.astype(jnp.bfloat16)


def group_attention(projected, prior, cache, lengths, offset, pre_rows, head_dim):
    part_count = projected.shape[0]
    pre_part = projected[:, :pre_rows].reshape((-1,) + projected.shape[2:])
    dec_part = projected[:, pre_rows:].reshape((-1,) + projected.shape[2:])
    pre_pos = (offset + jnp.arange(pre_part.shape[0], dtype=jnp.int32)).astype(jnp.float32)
    dec_pos = lengths.astype(jnp.float32)
    queries, key_rows, value_rows = split_heads(pre_part, pre_pos, head_dim)
    pre_out = prefill_attention(queries, key_rows, value_rows, prior, offset)
    queries, key_rows, value_rows = split_heads(dec_part, dec_pos, head_dim)
    dec_out = decode_attention(queries, key_rows, value_rows, cache, lengths)
    columns = pre_out.shape[1] * pre_out.shape[2] * pre_out.shape[3]
    pre_out = pre_out.reshape(part_count, pre_rows, columns)
    dec_out = dec_out.reshape(part_count, -1, columns)
    return jnp.concatenate([pre_out, dec_out], axis=1).reshape(-1, columns)


def pair_over(shard, axis):
    if lax.axis_size(axis) == 1:
        return shard[None]
    other = lax.ppermute(shard, axis, [(0, 1), (1, 0)])
    first = lax.axis_index(axis) == 0
    return jnp.stack([jnp.where(first, shard, other), jnp.where(first, other, shard)])


def across_halves(shard):
    return pair_over(shard, "zh")


def local(
    pre_tokens,
    dec_tokens,
    deal_slots,
    dec_lengths,
    pre_offsets,
    dec_cache,
    prior_cache,
    attn_gain,
    moe_gain,
    qkv_weight,
    out_weight,
    gate_up,
    down_weight,
    routes,
    route_gates,
):
    dp = ("zh", *DL)
    halves = lax.axis_size("zh")
    half_size = lax.axis_size("dc") * lax.axis_size("core")
    group_count = halves * half_size
    part_count = lax.axis_size("mp")
    group_index = (
        lax.axis_index("zh") * lax.axis_size("dc") + lax.axis_index("dc")
    ) * lax.axis_size("core") + lax.axis_index("core")
    part_index = lax.axis_index("mp")
    pre_rows = pre_tokens.shape[0]
    width = pre_tokens.shape[1]
    dec_rows = dec_tokens.shape[0]
    head_dim = dec_cache.shape[-1] // 2
    bundle = max(1, dec_rows // group_count)
    device = group_index * part_count + part_index
    position = jnp.arange(dec_rows, dtype=jnp.int32)
    own_deal = lax.dynamic_slice_in_dim(deal_slots, device * dec_rows, dec_rows, 0)
    target = own_deal // (part_count * dec_rows)
    group_ids = jnp.arange(group_count, dtype=jnp.int32)
    lane_ids = jnp.arange(bundle, dtype=jnp.int32)
    send_table = (
        (target[None, None, :] == group_ids[:, None, None])
        & (position[None, None, :] % bundle == lane_ids[None, :, None])
    ).astype(jnp.bfloat16)
    outgoing = jnp.einsum(
        "jbi,id->jbd", send_table, dec_tokens, preferred_element_type=jnp.float32
    ).astype(jnp.bfloat16)
    incoming = lax.all_to_all(outgoing, dp, split_axis=0, concat_axis=0, tiled=True)
    slot_ids = device * dec_rows + position
    request_ids = jnp.arange(deal_slots.shape[0], dtype=jnp.int32)
    request = jnp.sum(
        jnp.where(deal_slots[None, :] == slot_ids[:, None], request_ids[None, :], 0), axis=1
    )
    source = request // (part_count * dec_rows)
    lane = request % dec_rows % bundle
    take_table = (
        (source[:, None, None] == group_ids[None, :, None])
        & (lane[:, None, None] == lane_ids[None, None, :])
    ).astype(jnp.bfloat16)
    slot_rows = jnp.einsum(
        "ijb,jbd->id", take_table, incoming, preferred_element_type=jnp.float32
    ).astype(jnp.bfloat16)
    layer_input = jnp.concatenate([pre_tokens, slot_rows], axis=0)
    rows_dev = layer_input.shape[0]
    normed = root_norm(layer_input.astype(jnp.float32), attn_gain).astype(jnp.bfloat16)
    group_rows = lax.all_gather(normed, "mp", axis=0, tiled=True)
    local_width = qkv_weight.shape[1]
    qkv_pair = across_halves(qkv_weight)
    out_pair = jnp.moveaxis(across_halves(out_weight), 0, 1)
    qkv_full = pair_over(lax.all_gather(qkv_pair, "dc", axis=0, tiled=False), "core")
    qkv_full = jnp.transpose(qkv_full, (2, 1, 0, 3, 4)).reshape(-1, local_width)
    qkv_full, out_pair = lax.optimization_barrier((qkv_full, out_pair))
    projected = jnp.dot(group_rows, qkv_full, preferred_element_type=jnp.float32)
    local_groups = dec_cache.shape[0]
    projected = projected.reshape(part_count, rows_dev, local_groups, local_width // local_groups)
    attn_out = group_attention(
        projected, prior_cache[:, 0], dec_cache, dec_lengths, pre_offsets[0], pre_rows, head_dim
    )
    out_full = pair_over(lax.all_gather(out_pair, "dc", axis=1, tiled=False), "core")
    out_full = jnp.transpose(out_full, (1, 3, 2, 0, 4)).reshape(out_weight.shape[0], -1)
    partial_sums = jnp.dot(attn_out, out_full, preferred_element_type=jnp.float32)
    attn_sum = lax.psum_scatter(
        partial_sums.astype(jnp.bfloat16), "mp", scatter_dimension=0, tiled=True
    ).astype(jnp.float32)
    residual = layer_input.astype(jnp.float32) + attn_sum
    normed_moe = root_norm(residual, moe_gain).astype(jnp.bfloat16)
    expert_count = gate_up.shape[0]
    local_experts = max(1, expert_count // half_size)
    copies = max(1, half_size // expert_count)

    def owner_major(weights):
        per_half = jnp.repeat(weights, copies, axis=0).reshape(
            (half_size, local_experts) + weights.shape[1:]
        )
        both = jnp.broadcast_to(per_half[None], (halves,) + per_half.shape)
        return both.reshape((group_count, local_experts) + weights.shape[1:])

    gu_rows = gate_up.shape[1]
    owned = lax.all_to_all(
        jnp.concatenate([owner_major(gate_up), owner_major(down_weight)], axis=2),
        dp, split_axis=0, concat_axis=0, tiled=True,
    )
    owned_gu = jnp.moveaxis(owned[:, :, :gu_rows], 0, 1).reshape(
        (1, local_experts, -1) + gate_up.shape[2:]
    )
    owned_dn = jnp.moveaxis(owned[:, :, gu_rows:], 0, 1).reshape(
        (1, local_experts, -1) + down_weight.shape[2:]
    )
    full_gu, full_dn = (
        lax.all_gather(owned_gu, "mp", axis=3, tiled=True),
        lax.all_gather(owned_dn, "mp", axis=3, tiled=True),
    )
    full_gu = full_gu[0]
    full_dn = full_dn[0]
    topk = routes.shape[1]
    capacity = 4 * ((rows_dev * topk + 3 * expert_count - 1) // (3 * expert_count))
    expert_ids = jnp.arange(expert_count, dtype=jnp.int32)
    hits = routes[:, :, None] == expert_ids[None, None, :]
    chosen = jnp.any(hits, axis=1)
    weight = jnp.sum(jnp.where(hits, route_gates.astype(jnp.float32)[:, :, None], 0.0), axis=1)
    rank = jnp.cumsum(chosen.astype(jnp.int32), axis=0) - 1
    slot_range = jnp.arange(capacity, dtype=jnp.int32)
    placed = chosen.T[:, None, :] & (rank.T[:, None, :] == slot_range[None, :, None])
    combine_table = (placed.astype(jnp.float32) * weight.T[:, None, :]).astype(jnp.bfloat16)
    halfway = full_gu.shape[-1] // 2
    if copies > 1:
        chunks = [(slice(None), 0)]
    else:
        chunks = [(slice(l, None, local_experts), l) for l in range(local_experts)]
    moe_sum = jnp.zeros((rows_dev, width), jnp.float32)
    for picked, l in chunks:
        table = placed[picked].astype(jnp.bfloat16)
        outbound = jnp.einsum(
            "ecr,rd->ecd", table, normed_moe, preferred_element_type=jnp.float32
        ).astype(jnp.bfloat16)
        outbound = outbound.reshape(half_size, -1, width)
        arrived = lax.all_to_all(outbound, DL, split_axis=0, concat_axis=0, tiled=True)
        both = jnp.einsum(
            "snd,df->snf", arrived, full_gu[l], preferred_element_type=jnp.float32
        )
        activation = (jax.nn.silu(both[..., :halfway]) * both[..., halfway:]).astype(jnp.bfloat16)
        expert_out = jnp.einsum(
            "snf,fd->snd", activation, full_dn[l], preferred_element_type=jnp.float32
        ).astype(jnp.bfloat16)
        returned = lax.all_to_all(expert_out, DL, split_axis=0, concat_axis=0, tiled=True)
        returned = returned.reshape(-1, capacity, width)
        moe_sum = moe_sum + jnp.einsum(
            "ecr,ecd->rd", combine_table[picked], returned, preferred_element_type=jnp.float32
        )
    return (residual + moe_sum).astype(jnp.bfloat16)


def solution(mesh):
    groups = mesh.shape["dp"]
    halves = 2 if groups % 2 == 0 else 1
    cores = 2 if groups % (2 * halves) == 0 else 1
    devices = mesh.devices.reshape(halves, groups // halves // cores, cores, mesh.shape["mp"])
    split_mesh = jax.sharding.Mesh(devices, ("zh", "dc", "core", "mp"))
    dp = ("zh", *DL)
    return jax.shard_map(
        local,
        mesh=split_mesh,
        in_specs=(
            P((*dp, "mp"), None),
            P((*dp, "mp"), None),
            P(),
            P(dp),
            P(dp),
            P("mp", dp, None, None),
            P("mp", dp, None, None),
            P(),
            P(),
            P(dp, "mp"),
            P("mp", dp),
            P(None, dp, "mp"),
            P(None, dp, "mp"),
            P((*dp, "mp"), None),
            P((*dp, "mp"), None),
        ),
        out_specs=P((*dp, "mp"), None),
        check_vma=False,
    )
```

```python
import jax
import jax.numpy as jnp
from jax import lax
from jax.sharding import PartitionSpec as P

EPSILON = 1e-06
ROTARY_BASE = 10000.0
SCORE_SCALE = 0.015625
DL = ("dc", "core")


def root_norm(values, gain):
    mean_square = jnp.mean(values * values, axis=-1, keepdims=True)
    return values * lax.rsqrt(mean_square + EPSILON) * gain


def rotary(vectors, positions):
    halfway = vectors.shape[-1] // 2
    freq_table = ROTARY_BASE ** (-jnp.arange(halfway).astype(jnp.float32) / halfway)
    angles = positions[..., None] * freq_table
    cosine = jnp.cos(angles)
    sine_part = jnp.sin(angles)
    leading = vectors[..., :halfway]
    trailing = vectors[..., halfway:]
    return jnp.concatenate(
        [leading * cosine - trailing * sine_part, trailing * cosine + leading * sine_part], axis=-1
    )


def split_heads(projected, positions, head_dim):
    per_group = projected.shape[-1] // head_dim - 2
    row_count = projected.shape[0]
    group_count = projected.shape[1]
    queries = projected[..., : per_group * head_dim].reshape(
        row_count, group_count, per_group, head_dim
    )
    key_rows = projected[..., per_group * head_dim : (per_group + 1) * head_dim]
    value_rows = projected[..., (per_group + 1) * head_dim :]
    queries = rotary(queries, positions[:, None, None]).astype(jnp.bfloat16)
    key_rows = rotary(key_rows, positions[:, None]).astype(jnp.bfloat16)
    return (queries, key_rows, value_rows.astype(jnp.bfloat16))


def prefill_attention(queries, key_rows, value_rows, prior, offset):
    head_dim = queries.shape[-1]
    row_count = queries.shape[0]
    span = prior.shape[1]
    all_keys = jnp.concatenate([prior[:, :, :head_dim], jnp.swapaxes(key_rows, 0, 1)], axis=1)
    all_values = jnp.concatenate([prior[:, :, head_dim:], jnp.swapaxes(value_rows, 0, 1)], axis=1)
    scores = (
        jnp.einsum("cgph,gkh->gpck", queries, all_keys, preferred_element_type=jnp.float32)
        * SCORE_SCALE
    )
    column = jnp.arange(span + row_count)
    row_ids = jnp.arange(row_count)
    allowed = jnp.where(
        column[None, :] < span, column[None, :] < offset, column[None, :] - span <= row_ids[:, None]
    )
    scores = jnp.where(allowed, scores, -jnp.inf)
    highest = jnp.max(scores, axis=-1, keepdims=True)
    expo = jnp.exp(scores - highest)
    weights = (expo / jnp.sum(expo, axis=-1, keepdims=True)).astype(jnp.bfloat16)
    mixed = jnp.einsum("gpck,gkh->cgph", weights, all_values, preferred_element_type=jnp.float32)
    return mixed.astype(jnp.bfloat16)


def decode_attention(queries, key_rows, value_rows, cache, lengths):
    head_dim = queries.shape[-1]
    cached = (
        jnp.einsum(
            "sgph,gslh->sgpl", queries, cache[..., :head_dim], preferred_element_type=jnp.float32
        )
        * SCORE_SCALE
    )
    own_score = (
        jnp.einsum("sgph,sgh->sgp", queries, key_rows, preferred_element_type=jnp.float32)
        * SCORE_SCALE
    )
    valid = jnp.arange(cache.shape[2])[None, :] < lengths[:, None]
    cached = jnp.where(valid[:, None, None, :], cached, -jnp.inf)
    highest = jnp.maximum(jnp.max(cached, axis=-1), own_score)
    expo = jnp.exp(cached - highest[..., None])
    own_expo = jnp.exp(own_score - highest)
    total = jnp.sum(expo, axis=-1) + own_expo
    weights = (expo / total[..., None]).astype(jnp.bfloat16)
    own_weight = (own_expo / total).astype(jnp.bfloat16)
    mixed = jnp.einsum(
        "sgpl,gslh->sgph", weights, cache[..., head_dim:], preferred_element_type=jnp.float32
    )
    mixed = (
        mixed
        + own_weight.astype(jnp.float32)[..., None] * value_rows.astype(jnp.float32)[:, :, None, :]
    )
    return mixed.astype(jnp.bfloat16)


def group_attention(projected, prior, cache, lengths, offset, pre_rows, head_dim):
    part_count = projected.shape[0]
    pre_part = projected[:, :pre_rows].reshape((-1,) + projected.shape[2:])
    dec_part = projected[:, pre_rows:].reshape((-1,) + projected.shape[2:])
    pre_pos = (offset + jnp.arange(pre_part.shape[0], dtype=jnp.int32)).astype(jnp.float32)
    dec_pos = lengths.astype(jnp.float32)
    queries, key_rows, value_rows = split_heads(pre_part, pre_pos, head_dim)
    pre_out = prefill_attention(queries, key_rows, value_rows, prior, offset)
    queries, key_rows, value_rows = split_heads(dec_part, dec_pos, head_dim)
    dec_out = decode_attention(queries, key_rows, value_rows, cache, lengths)
    columns = pre_out.shape[1] * pre_out.shape[2] * pre_out.shape[3]
    pre_out = pre_out.reshape(part_count, pre_rows, columns)
    dec_out = dec_out.reshape(part_count, -1, columns)
    return jnp.concatenate([pre_out, dec_out], axis=1).reshape(-1, columns)


def pair_over(shard, axis):
    if lax.axis_size(axis) == 1:
        return shard[None]
    other = lax.ppermute(shard, axis, [(0, 1), (1, 0)])
    first = lax.axis_index(axis) == 0
    return jnp.stack([jnp.where(first, shard, other), jnp.where(first, other, shard)])


def across_halves(shard):
    return pair_over(shard, "zh")


def local(
    pre_tokens,
    dec_tokens,
    deal_slots,
    dec_lengths,
    pre_offsets,
    dec_cache,
    prior_cache,
    attn_gain,
    moe_gain,
    qkv_weight,
    out_weight,
    gate_up,
    down_weight,
    routes,
    route_gates,
):
    dp = ("zh", *DL)
    halves = lax.axis_size("zh")
    half_size = lax.axis_size("dc") * lax.axis_size("core")
    group_count = halves * half_size
    part_count = lax.axis_size("mp")
    group_index = (
        lax.axis_index("zh") * lax.axis_size("dc") + lax.axis_index("dc")
    ) * lax.axis_size("core") + lax.axis_index("core")
    part_index = lax.axis_index("mp")
    pre_rows = pre_tokens.shape[0]
    width = pre_tokens.shape[1]
    dec_rows = dec_tokens.shape[0]
    head_dim = dec_cache.shape[-1] // 2
    bundle = max(1, dec_rows // group_count)
    device = group_index * part_count + part_index
    position = jnp.arange(dec_rows, dtype=jnp.int32)
    slot_ids = device * dec_rows + position
    take_table = (deal_slots[None, :] == slot_ids[:, None]).astype(jnp.bfloat16)
    every_request = pair_over(
        lax.all_gather(pair_over(dec_tokens, "zh"), "dc", axis=0, tiled=False), "core"
    )
    every_request = jnp.transpose(every_request, (2, 1, 0, 3, 4)).reshape(
        group_count, dec_rows, width
    )
    every_request = lax.all_gather(every_request, "mp", axis=1, tiled=False).reshape(-1, width)
    slot_rows = jnp.dot(
        take_table, every_request, preferred_element_type=jnp.float32
    ).astype(jnp.bfloat16)
    layer_input = jnp.concatenate([pre_tokens, slot_rows], axis=0)
    rows_dev = layer_input.shape[0]
    normed = root_norm(layer_input.astype(jnp.float32), attn_gain).astype(jnp.bfloat16)
    group_rows = lax.all_gather(normed, "mp", axis=0, tiled=True)
    local_width = qkv_weight.shape[1]
    qkv_pair = across_halves(qkv_weight)
    out_pair = jnp.moveaxis(across_halves(out_weight), 0, 1)
    qkv_full = pair_over(lax.all_gather(qkv_pair, "dc", axis=0, tiled=False), "core")
    qkv_full = jnp.transpose(qkv_full, (2, 1, 0, 3, 4)).reshape(-1, local_width)
    qkv_full, out_pair = lax.optimization_barrier((qkv_full, out_pair))
    projected = jnp.dot(group_rows, qkv_full, preferred_element_type=jnp.float32)
    local_groups = dec_cache.shape[0]
    projected = projected.reshape(part_count, rows_dev, local_groups, local_width // local_groups)
    attn_out = group_attention(
        projected, prior_cache[:, 0], dec_cache, dec_lengths, pre_offsets[0], pre_rows, head_dim
    )
    out_full = pair_over(lax.all_gather(out_pair, "dc", axis=1, tiled=False), "core")
    out_full = jnp.transpose(out_full, (1, 3, 2, 0, 4)).reshape(out_weight.shape[0], -1)
    partial_sums = jnp.dot(attn_out, out_full, preferred_element_type=jnp.float32)
    attn_sum = lax.psum_scatter(
        partial_sums.astype(jnp.bfloat16), "mp", scatter_dimension=0, tiled=True
    ).astype(jnp.float32)
    residual = layer_input.astype(jnp.float32) + attn_sum
    normed_moe = root_norm(residual, moe_gain).astype(jnp.bfloat16)
    expert_count = gate_up.shape[0]
    local_experts = max(1, expert_count // half_size)
    copies = max(1, half_size // expert_count)

    def owner_major(weights):
        per_half = jnp.repeat(weights, copies, axis=0).reshape(
            (half_size, local_experts) + weights.shape[1:]
        )
        both = jnp.broadcast_to(per_half[None], (halves,) + per_half.shape)
        return both.reshape((group_count, local_experts) + weights.shape[1:])

    gu_rows = gate_up.shape[1]
    owned = lax.all_to_all(
        jnp.concatenate([owner_major(gate_up), owner_major(down_weight)], axis=2),
        dp, split_axis=0, concat_axis=0, tiled=True,
    )
    owned_gu = jnp.moveaxis(owned[:, :, :gu_rows], 0, 1).reshape(
        (1, local_experts, -1) + gate_up.shape[2:]
    )
    owned_dn = jnp.moveaxis(owned[:, :, gu_rows:], 0, 1).reshape(
        (1, local_experts, -1) + down_weight.shape[2:]
    )
    full_gu, full_dn = (
        lax.all_gather(owned_gu, "mp", axis=3, tiled=True),
        lax.all_gather(owned_dn, "mp", axis=3, tiled=True),
    )
    full_gu = full_gu[0]
    full_dn = full_dn[0]
    topk = routes.shape[1]
    capacity = 4 * ((rows_dev * topk + 3 * expert_count - 1) // (3 * expert_count))
    expert_ids = jnp.arange(expert_count, dtype=jnp.int32)
    hits = routes[:, :, None] == expert_ids[None, None, :]
    chosen = jnp.any(hits, axis=1)
    weight = jnp.sum(jnp.where(hits, route_gates.astype(jnp.float32)[:, :, None], 0.0), axis=1)
    rank = jnp.cumsum(chosen.astype(jnp.int32), axis=0) - 1
    slot_range = jnp.arange(capacity, dtype=jnp.int32)
    placed = chosen.T[:, None, :] & (rank.T[:, None, :] == slot_range[None, :, None])
    combine_table = (placed.astype(jnp.float32) * weight.T[:, None, :]).astype(jnp.bfloat16)
    halfway = full_gu.shape[-1] // 2
    if copies > 1:
        chunks = [(slice(None), 0)]
    else:
        chunks = [(slice(l, None, local_experts), l) for l in range(local_experts)]
    moe_sum = jnp.zeros((rows_dev, width), jnp.float32)
    for picked, l in chunks:
        table = placed[picked].astype(jnp.bfloat16)
        outbound = jnp.einsum(
            "ecr,rd->ecd", table, normed_moe, preferred_element_type=jnp.float32
        ).astype(jnp.bfloat16)
        outbound = outbound.reshape(half_size, -1, width)
        arrived = lax.all_to_all(outbound, DL, split_axis=0, concat_axis=0, tiled=True)
        both = jnp.einsum(
            "snd,df->snf", arrived, full_gu[l], preferred_element_type=jnp.float32
        )
        activation = (jax.nn.silu(both[..., :halfway]) * both[..., halfway:]).astype(jnp.bfloat16)
        expert_out = jnp.einsum(
            "snf,fd->snd", activation, full_dn[l], preferred_element_type=jnp.float32
        ).astype(jnp.bfloat16)
        returned = lax.all_to_all(expert_out, DL, split_axis=0, concat_axis=0, tiled=True)
        returned = returned.reshape(-1, capacity, width)
        moe_sum = moe_sum + jnp.einsum(
            "ecr,ecd->rd", combine_table[picked], returned, preferred_element_type=jnp.float32
        )
    return (residual + moe_sum).astype(jnp.bfloat16)


def solution(mesh):
    groups = mesh.shape["dp"]
    halves = 2 if groups % 2 == 0 else 1
    cores = 2 if groups % (2 * halves) == 0 else 1
    devices = mesh.devices.reshape(halves, groups // halves // cores, cores, mesh.shape["mp"])
    split_mesh = jax.sharding.Mesh(devices, ("zh", "dc", "core", "mp"))
    dp = ("zh", *DL)
    return jax.shard_map(
        local,
        mesh=split_mesh,
        in_specs=(
            P((*dp, "mp"), None),
            P((*dp, "mp"), None),
            P(),
            P(dp),
            P(dp),
            P("mp", dp, None, None),
            P("mp", dp, None, None),
            P(),
            P(),
            P(dp, "mp"),
            P("mp", dp),
            P(None, dp, "mp"),
            P(None, dp, "mp"),
            P((*dp, "mp"), None),
            P((*dp, "mp"), None),
        ),
        out_specs=P((*dp, "mp"), None),
        check_vma=False,
    )
```

```python
import jax
import jax.numpy as jnp
from jax import lax
from jax.sharding import PartitionSpec as P

EPSILON = 1e-06
ROTARY_BASE = 10000.0
SCORE_SCALE = 0.015625


def root_norm(values, gain):
    mean_square = jnp.mean(values * values, axis=-1, keepdims=True)
    return values * lax.rsqrt(mean_square + EPSILON) * gain


def rotary(vectors, positions):
    halfway = vectors.shape[-1] // 2
    freq_table = ROTARY_BASE ** (-jnp.arange(halfway).astype(jnp.float32) / halfway)
    angles = positions[..., None] * freq_table
    cosine = jnp.cos(angles)
    sine_part = jnp.sin(angles)
    leading = vectors[..., :halfway]
    trailing = vectors[..., halfway:]
    return jnp.concatenate(
        [leading * cosine - trailing * sine_part, trailing * cosine + leading * sine_part], axis=-1
    )


def split_heads(projected, positions, head_dim):
    per_group = projected.shape[-1] // head_dim - 2
    row_count = projected.shape[0]
    group_count = projected.shape[1]
    queries = projected[..., : per_group * head_dim].reshape(
        row_count, group_count, per_group, head_dim
    )
    key_rows = projected[..., per_group * head_dim : (per_group + 1) * head_dim]
    value_rows = projected[..., (per_group + 1) * head_dim :]
    queries = rotary(queries, positions[:, None, None]).astype(jnp.bfloat16)
    key_rows = rotary(key_rows, positions[:, None]).astype(jnp.bfloat16)
    return (queries, key_rows, value_rows.astype(jnp.bfloat16))


def prefill_attention(queries, key_rows, value_rows, prior, offset):
    head_dim = queries.shape[-1]
    row_count = queries.shape[0]
    span = prior.shape[1]
    all_keys = jnp.concatenate([prior[:, :, :head_dim], jnp.swapaxes(key_rows, 0, 1)], axis=1)
    all_values = jnp.concatenate([prior[:, :, head_dim:], jnp.swapaxes(value_rows, 0, 1)], axis=1)
    scores = (
        jnp.einsum("cgph,gkh->gpck", queries, all_keys, preferred_element_type=jnp.float32)
        * SCORE_SCALE
    )
    column = jnp.arange(span + row_count)
    row_ids = jnp.arange(row_count)
    allowed = jnp.where(
        column[None, :] < span, column[None, :] < offset, column[None, :] - span <= row_ids[:, None]
    )
    scores = jnp.where(allowed, scores, -jnp.inf)
    highest = jnp.max(scores, axis=-1, keepdims=True)
    expo = jnp.exp(scores - highest)
    weights = (expo / jnp.sum(expo, axis=-1, keepdims=True)).astype(jnp.bfloat16)
    mixed = jnp.einsum("gpck,gkh->cgph", weights, all_values, preferred_element_type=jnp.float32)
    return mixed.astype(jnp.bfloat16)


def decode_attention(queries, key_rows, value_rows, cache, lengths):
    head_dim = queries.shape[-1]
    cached = (
        jnp.einsum(
            "sgph,gslh->sgpl", queries, cache[..., :head_dim], preferred_element_type=jnp.float32
        )
        * SCORE_SCALE
    )
    own_score = (
        jnp.einsum("sgph,sgh->sgp", queries, key_rows, preferred_element_type=jnp.float32)
        * SCORE_SCALE
    )
    valid = jnp.arange(cache.shape[2])[None, :] < lengths[:, None]
    cached = jnp.where(valid[:, None, None, :], cached, -jnp.inf)
    highest = jnp.maximum(jnp.max(cached, axis=-1), own_score)
    expo = jnp.exp(cached - highest[..., None])
    own_expo = jnp.exp(own_score - highest)
    total = jnp.sum(expo, axis=-1) + own_expo
    weights = (expo / total[..., None]).astype(jnp.bfloat16)
    own_weight = (own_expo / total).astype(jnp.bfloat16)
    mixed = jnp.einsum(
        "sgpl,gslh->sgph", weights, cache[..., head_dim:], preferred_element_type=jnp.float32
    )
    mixed = (
        mixed
        + own_weight.astype(jnp.float32)[..., None] * value_rows.astype(jnp.float32)[:, :, None, :]
    )
    return mixed.astype(jnp.bfloat16)


def group_attention(projected, prior, cache, lengths, offset, pre_rows, head_dim):
    part_count = projected.shape[0]
    pre_part = projected[:, :pre_rows].reshape((-1,) + projected.shape[2:])
    dec_part = projected[:, pre_rows:].reshape((-1,) + projected.shape[2:])
    pre_pos = (offset + jnp.arange(pre_part.shape[0], dtype=jnp.int32)).astype(jnp.float32)
    dec_pos = lengths.astype(jnp.float32)
    queries, key_rows, value_rows = split_heads(pre_part, pre_pos, head_dim)
    pre_out = prefill_attention(queries, key_rows, value_rows, prior, offset)
    queries, key_rows, value_rows = split_heads(dec_part, dec_pos, head_dim)
    dec_out = decode_attention(queries, key_rows, value_rows, cache, lengths)
    columns = pre_out.shape[1] * pre_out.shape[2] * pre_out.shape[3]
    pre_out = pre_out.reshape(part_count, pre_rows, columns)
    dec_out = dec_out.reshape(part_count, -1, columns)
    return jnp.concatenate([pre_out, dec_out], axis=1).reshape(-1, columns)


def across_halves(shard):
    halves = lax.axis_size("zh")
    if halves == 1:
        return shard[None]
    other = lax.ppermute(shard, "zh", [(0, 1), (1, 0)])
    first = lax.axis_index("zh") == 0
    return jnp.stack([jnp.where(first, shard, other), jnp.where(first, other, shard)])


def exchange(blocks, axis):
    size = blocks.shape[0]
    me = lax.axis_index(axis)
    arrived = [lax.dynamic_index_in_dim(blocks, me, 0, keepdims=False)]
    for shift in range(1, size):
        sent = lax.dynamic_index_in_dim(blocks, (me + shift) % size, 0, keepdims=False)
        pairs = [(i, (i + shift) % size) for i in range(size)]
        arrived.append(lax.ppermute(sent, axis, pairs))
    order = (me - jnp.arange(size, dtype=jnp.int32)) % size
    return jnp.take(jnp.stack(arrived), order, axis=0)


def local(
    pre_tokens,
    dec_tokens,
    deal_slots,
    dec_lengths,
    pre_offsets,
    dec_cache,
    prior_cache,
    attn_gain,
    moe_gain,
    qkv_weight,
    out_weight,
    gate_up,
    down_weight,
    routes,
    route_gates,
):
    dp = ("zh", "dl")
    halves = lax.axis_size("zh")
    half_size = lax.axis_size("dl")
    group_count = halves * half_size
    part_count = lax.axis_size("mp")
    group_index = lax.axis_index("zh") * half_size + lax.axis_index("dl")
    part_index = lax.axis_index("mp")
    pre_rows = pre_tokens.shape[0]
    width = pre_tokens.shape[1]
    dec_rows = dec_tokens.shape[0]
    head_dim = dec_cache.shape[-1] // 2
    bundle = max(1, dec_rows // group_count)
    device = group_index * part_count + part_index
    position = jnp.arange(dec_rows, dtype=jnp.int32)
    own_deal = lax.dynamic_slice_in_dim(deal_slots, device * dec_rows, dec_rows, 0)
    target = own_deal // (part_count * dec_rows)
    group_ids = jnp.arange(group_count, dtype=jnp.int32)
    lane_ids = jnp.arange(bundle, dtype=jnp.int32)
    send_table = (
        (target[None, None, :] == group_ids[:, None, None])
        & (position[None, None, :] % bundle == lane_ids[None, :, None])
    ).astype(jnp.bfloat16)
    outgoing = jnp.einsum(
        "jbi,id->jbd", send_table, dec_tokens, preferred_element_type=jnp.float32
    ).astype(jnp.bfloat16)
    incoming = lax.all_to_all(outgoing, dp, split_axis=0, concat_axis=0, tiled=True)
    slot_ids = device * dec_rows + position
    request_ids = jnp.arange(deal_slots.shape[0], dtype=jnp.int32)
    request = jnp.sum(
        jnp.where(deal_slots[None, :] == slot_ids[:, None], request_ids[None, :], 0), axis=1
    )
    source = request // (part_count * dec_rows)
    lane = request % dec_rows % bundle
    take_table = (
        (source[:, None, None] == group_ids[None, :, None])
        & (lane[:, None, None] == lane_ids[None, None, :])
    ).astype(jnp.bfloat16)
    slot_rows = jnp.einsum(
        "ijb,jbd->id", take_table, incoming, preferred_element_type=jnp.float32
    ).astype(jnp.bfloat16)
    layer_input = jnp.concatenate([pre_tokens, slot_rows], axis=0)
    rows_dev = layer_input.shape[0]
    normed = root_norm(layer_input.astype(jnp.float32), attn_gain).astype(jnp.bfloat16)
    group_rows = lax.all_gather(normed, "mp", axis=0, tiled=True)
    local_width = qkv_weight.shape[1]
    qkv_pair = across_halves(qkv_weight)
    out_pair = jnp.moveaxis(across_halves(out_weight), 0, 1)
    qkv_full = lax.all_gather(qkv_pair, "dl", axis=0, tiled=False)
    qkv_full = jnp.swapaxes(qkv_full, 0, 1).reshape(-1, local_width)
    qkv_full, out_pair = lax.optimization_barrier((qkv_full, out_pair))
    projected = jnp.dot(group_rows, qkv_full, preferred_element_type=jnp.float32)
    local_groups = dec_cache.shape[0]
    projected = projected.reshape(part_count, rows_dev, local_groups, local_width // local_groups)
    attn_out = group_attention(
        projected, prior_cache[:, 0], dec_cache, dec_lengths, pre_offsets[0], pre_rows, head_dim
    )
    out_full = lax.all_gather(out_pair, "dl", axis=1, tiled=False)
    out_full = jnp.swapaxes(out_full, 1, 2).reshape(out_weight.shape[0], -1)
    partial_sums = jnp.dot(attn_out, out_full, preferred_element_type=jnp.float32)
    attn_sum = lax.psum_scatter(
        partial_sums.astype(jnp.bfloat16), "mp", scatter_dimension=0, tiled=True
    ).astype(jnp.float32)
    residual = layer_input.astype(jnp.float32) + attn_sum
    normed_moe = root_norm(residual, moe_gain).astype(jnp.bfloat16)
    expert_count = gate_up.shape[0]
    local_experts = max(1, expert_count // half_size)
    copies = max(1, half_size // expert_count)

    def owner_major(weights):
        per_half = jnp.repeat(weights, copies, axis=0).reshape(
            (half_size, local_experts) + weights.shape[1:]
        )
        both = jnp.broadcast_to(per_half[None], (halves,) + per_half.shape)
        return both.reshape((group_count, local_experts) + weights.shape[1:])

    gu_rows = gate_up.shape[1]
    owned = lax.all_to_all(
        jnp.concatenate([owner_major(gate_up), owner_major(down_weight)], axis=2),
        dp, split_axis=0, concat_axis=0, tiled=True,
    )
    owned_gu = jnp.moveaxis(owned[:, :, :gu_rows], 0, 1).reshape(
        (1, local_experts, -1) + gate_up.shape[2:]
    )
    owned_dn = jnp.moveaxis(owned[:, :, gu_rows:], 0, 1).reshape(
        (1, local_experts, -1) + down_weight.shape[2:]
    )
    full_gu, full_dn = (
        lax.all_gather(owned_gu, "mp", axis=3, tiled=True),
        lax.all_gather(owned_dn, "mp", axis=3, tiled=True),
    )
    full_gu = full_gu[0]
    full_dn = full_dn[0]
    topk = routes.shape[1]
    capacity = 4 * ((rows_dev * topk + 3 * expert_count - 1) // (3 * expert_count))
    expert_ids = jnp.arange(expert_count, dtype=jnp.int32)
    hits = routes[:, :, None] == expert_ids[None, None, :]
    chosen = jnp.any(hits, axis=1)
    weight = jnp.sum(jnp.where(hits, route_gates.astype(jnp.float32)[:, :, None], 0.0), axis=1)
    rank = jnp.cumsum(chosen.astype(jnp.int32), axis=0) - 1
    slot_range = jnp.arange(capacity, dtype=jnp.int32)
    placed = chosen.T[:, None, :] & (rank.T[:, None, :] == slot_range[None, :, None])
    combine_table = (placed.astype(jnp.float32) * weight.T[:, None, :]).astype(jnp.bfloat16)
    halfway = full_gu.shape[-1] // 2
    if copies > 1:
        chunks = [(slice(None), 0)]
    else:
        chunks = [(slice(l, None, local_experts), l) for l in range(local_experts)]
    moe_sum = jnp.zeros((rows_dev, width), jnp.float32)
    for picked, l in chunks:
        table = placed[picked].astype(jnp.bfloat16)
        outbound = jnp.einsum(
            "ecr,rd->ecd", table, normed_moe, preferred_element_type=jnp.float32
        ).astype(jnp.bfloat16)
        outbound = outbound.reshape(half_size, -1, width)
        arrived = exchange(outbound, "dl")
        both = jnp.einsum(
            "snd,df->snf", arrived, full_gu[l], preferred_element_type=jnp.float32
        )
        activation = (jax.nn.silu(both[..., :halfway]) * both[..., halfway:]).astype(jnp.bfloat16)
        expert_out = jnp.einsum(
            "snf,fd->snd", activation, full_dn[l], preferred_element_type=jnp.float32
        ).astype(jnp.bfloat16)
        returned = exchange(expert_out, "dl")
        returned = returned.reshape(-1, capacity, width)
        moe_sum = moe_sum + jnp.einsum(
            "ecr,ecd->rd", combine_table[picked], returned, preferred_element_type=jnp.float32
        )
    return (residual + moe_sum).astype(jnp.bfloat16)


def solution(mesh):
    groups = mesh.shape["dp"]
    halves = 2 if groups % 2 == 0 else 1
    devices = mesh.devices.reshape(halves, groups // halves, mesh.shape["mp"])
    split_mesh = jax.sharding.Mesh(devices, ("zh", "dl", "mp"))
    dp = ("zh", "dl")
    return jax.shard_map(
        local,
        mesh=split_mesh,
        in_specs=(
            P((*dp, "mp"), None),
            P((*dp, "mp"), None),
            P(),
            P(dp),
            P(dp),
            P("mp", dp, None, None),
            P("mp", dp, None, None),
            P(),
            P(),
            P(dp, "mp"),
            P("mp", dp),
            P(None, dp, "mp"),
            P(None, dp, "mp"),
            P((*dp, "mp"), None),
            P((*dp, "mp"), None),
        ),
        out_specs=P((*dp, "mp"), None),
        check_vma=False,
    )
```

```python
import jax
import jax.numpy as jnp
from jax import lax
from jax.sharding import PartitionSpec as P

EPSILON = 1e-06
ROTARY_BASE = 10000.0
SCORE_SCALE = 0.015625
DL = ("dc", "core")


def root_norm(values, gain):
    mean_square = jnp.mean(values * values, axis=-1, keepdims=True)
    return values * lax.rsqrt(mean_square + EPSILON) * gain


def rotary(vectors, positions):
    halfway = vectors.shape[-1] // 2
    freq_table = ROTARY_BASE ** (-jnp.arange(halfway).astype(jnp.float32) / halfway)
    angles = positions[..., None] * freq_table
    cosine = jnp.cos(angles)
    sine_part = jnp.sin(angles)
    leading = vectors[..., :halfway]
    trailing = vectors[..., halfway:]
    return jnp.concatenate(
        [leading * cosine - trailing * sine_part, trailing * cosine + leading * sine_part], axis=-1
    )


def split_heads(projected, positions, head_dim):
    per_group = projected.shape[-1] // head_dim - 2
    row_count = projected.shape[0]
    group_count = projected.shape[1]
    queries = projected[..., : per_group * head_dim].reshape(
        row_count, group_count, per_group, head_dim
    )
    key_rows = projected[..., per_group * head_dim : (per_group + 1) * head_dim]
    value_rows = projected[..., (per_group + 1) * head_dim :]
    queries = rotary(queries, positions[:, None, None]).astype(jnp.bfloat16)
    key_rows = rotary(key_rows, positions[:, None]).astype(jnp.bfloat16)
    return (queries, key_rows, value_rows.astype(jnp.bfloat16))


def prefill_attention(queries, key_rows, value_rows, prior, offset):
    head_dim = queries.shape[-1]
    row_count = queries.shape[0]
    span = prior.shape[1]
    all_keys = jnp.concatenate([prior[:, :, :head_dim], jnp.swapaxes(key_rows, 0, 1)], axis=1)
    all_values = jnp.concatenate([prior[:, :, head_dim:], jnp.swapaxes(value_rows, 0, 1)], axis=1)
    scores = (
        jnp.einsum("cgph,gkh->gpck", queries, all_keys, preferred_element_type=jnp.float32)
        * SCORE_SCALE
    )
    column = jnp.arange(span + row_count)
    row_ids = jnp.arange(row_count)
    allowed = jnp.where(
        column[None, :] < span, column[None, :] < offset, column[None, :] - span <= row_ids[:, None]
    )
    scores = jnp.where(allowed, scores, -jnp.inf)
    highest = jnp.max(scores, axis=-1, keepdims=True)
    expo = jnp.exp(scores - highest)
    weights = (expo / jnp.sum(expo, axis=-1, keepdims=True)).astype(jnp.bfloat16)
    mixed = jnp.einsum("gpck,gkh->cgph", weights, all_values, preferred_element_type=jnp.float32)
    return mixed.astype(jnp.bfloat16)


def decode_attention(queries, key_rows, value_rows, cache, lengths):
    head_dim = queries.shape[-1]
    cached = (
        jnp.einsum(
            "sgph,gslh->sgpl", queries, cache[..., :head_dim], preferred_element_type=jnp.float32
        )
        * SCORE_SCALE
    )
    own_score = (
        jnp.einsum("sgph,sgh->sgp", queries, key_rows, preferred_element_type=jnp.float32)
        * SCORE_SCALE
    )
    valid = jnp.arange(cache.shape[2])[None, :] < lengths[:, None]
    cached = jnp.where(valid[:, None, None, :], cached, -jnp.inf)
    highest = jnp.maximum(jnp.max(cached, axis=-1), own_score)
    expo = jnp.exp(cached - highest[..., None])
    own_expo = jnp.exp(own_score - highest)
    total = jnp.sum(expo, axis=-1) + own_expo
    weights = (expo / total[..., None]).astype(jnp.bfloat16)
    own_weight = (own_expo / total).astype(jnp.bfloat16)
    mixed = jnp.einsum(
        "sgpl,gslh->sgph", weights, cache[..., head_dim:], preferred_element_type=jnp.float32
    )
    mixed = (
        mixed
        + own_weight.astype(jnp.float32)[..., None] * value_rows.astype(jnp.float32)[:, :, None, :]
    )
    return mixed.astype(jnp.bfloat16)


def group_attention(projected, prior, cache, lengths, offset, pre_rows, head_dim):
    part_count = projected.shape[0]
    pre_part = projected[:, :pre_rows].reshape((-1,) + projected.shape[2:])
    dec_part = projected[:, pre_rows:].reshape((-1,) + projected.shape[2:])
    pre_pos = (offset + jnp.arange(pre_part.shape[0], dtype=jnp.int32)).astype(jnp.float32)
    dec_pos = lengths.astype(jnp.float32)
    queries, key_rows, value_rows = split_heads(pre_part, pre_pos, head_dim)
    pre_out = prefill_attention(queries, key_rows, value_rows, prior, offset)
    queries, key_rows, value_rows = split_heads(dec_part, dec_pos, head_dim)
    dec_out = decode_attention(queries, key_rows, value_rows, cache, lengths)
    columns = pre_out.shape[1] * pre_out.shape[2] * pre_out.shape[3]
    pre_out = pre_out.reshape(part_count, pre_rows, columns)
    dec_out = dec_out.reshape(part_count, -1, columns)
    return jnp.concatenate([pre_out, dec_out], axis=1).reshape(-1, columns)


def pair_over(shard, axis):
    if lax.axis_size(axis) == 1:
        return shard[None]
    other = lax.ppermute(shard, axis, [(0, 1), (1, 0)])
    first = lax.axis_index(axis) == 0
    return jnp.stack([jnp.where(first, shard, other), jnp.where(first, other, shard)])


def across_halves(shard):
    return pair_over(shard, "zh")


def local(
    pre_tokens,
    dec_tokens,
    deal_slots,
    dec_lengths,
    pre_offsets,
    dec_cache,
    prior_cache,
    attn_gain,
    moe_gain,
    qkv_weight,
    out_weight,
    gate_up,
    down_weight,
    routes,
    route_gates,
):
    dp = ("zh", *DL)
    halves = lax.axis_size("zh")
    half_size = lax.axis_size("dc") * lax.axis_size("core")
    group_count = halves * half_size
    part_count = lax.axis_size("mp")
    group_index = (
        lax.axis_index("zh") * lax.axis_size("dc") + lax.axis_index("dc")
    ) * lax.axis_size("core") + lax.axis_index("core")
    part_index = lax.axis_index("mp")
    pre_rows = pre_tokens.shape[0]
    width = pre_tokens.shape[1]
    dec_rows = dec_tokens.shape[0]
    head_dim = dec_cache.shape[-1] // 2
    bundle = max(1, dec_rows // group_count)
    device = group_index * part_count + part_index
    position = jnp.arange(dec_rows, dtype=jnp.int32)
    own_deal = lax.dynamic_slice_in_dim(deal_slots, device * dec_rows, dec_rows, 0)
    target = own_deal // (part_count * dec_rows)
    group_ids = jnp.arange(group_count, dtype=jnp.int32)
    lane_ids = jnp.arange(bundle, dtype=jnp.int32)
    send_table = (
        (target[None, None, :] == group_ids[:, None, None])
        & (position[None, None, :] % bundle == lane_ids[None, :, None])
    ).astype(jnp.bfloat16)
    outgoing = jnp.einsum(
        "jbi,id->jbd", send_table, dec_tokens, preferred_element_type=jnp.float32
    ).astype(jnp.bfloat16)
    incoming = lax.all_to_all(outgoing, dp, split_axis=0, concat_axis=0, tiled=True)
    slot_ids = device * dec_rows + position
    request_ids = jnp.arange(deal_slots.shape[0], dtype=jnp.int32)
    request = jnp.sum(
        jnp.where(deal_slots[None, :] == slot_ids[:, None], request_ids[None, :], 0), axis=1
    )
    source = request // (part_count * dec_rows)
    lane = request % dec_rows % bundle
    take_table = (
        (source[:, None, None] == group_ids[None, :, None])
        & (lane[:, None, None] == lane_ids[None, None, :])
    ).astype(jnp.bfloat16)
    slot_rows = jnp.einsum(
        "ijb,jbd->id", take_table, incoming, preferred_element_type=jnp.float32
    ).astype(jnp.bfloat16)
    layer_input = jnp.concatenate([pre_tokens, slot_rows], axis=0)
    rows_dev = layer_input.shape[0]
    normed = root_norm(layer_input.astype(jnp.float32), attn_gain).astype(jnp.bfloat16)
    group_rows = lax.all_gather(normed, "mp", axis=0, tiled=True)
    local_width = qkv_weight.shape[1]
    qkv_pair = across_halves(qkv_weight)
    out_pair = jnp.moveaxis(across_halves(out_weight), 0, 1)
    qkv_full = lax.all_gather(qkv_pair, DL, axis=0, tiled=False)
    qkv_full = jnp.swapaxes(qkv_full, 0, 1).reshape(-1, local_width)
    qkv_full, out_pair = lax.optimization_barrier((qkv_full, out_pair))
    projected = jnp.dot(group_rows, qkv_full, preferred_element_type=jnp.float32)
    local_groups = dec_cache.shape[0]
    projected = projected.reshape(part_count, rows_dev, local_groups, local_width // local_groups)
    attn_out = group_attention(
        projected, prior_cache[:, 0], dec_cache, dec_lengths, pre_offsets[0], pre_rows, head_dim
    )
    out_full = pair_over(lax.all_gather(out_pair, "dc", axis=1, tiled=False), "core")
    out_full = jnp.transpose(out_full, (1, 3, 2, 0, 4)).reshape(out_weight.shape[0], -1)
    partial_sums = jnp.dot(attn_out, out_full, preferred_element_type=jnp.float32)
    attn_sum = lax.psum_scatter(
        partial_sums.astype(jnp.bfloat16), "mp", scatter_dimension=0, tiled=True
    ).astype(jnp.float32)
    residual = layer_input.astype(jnp.float32) + attn_sum
    normed_moe = root_norm(residual, moe_gain).astype(jnp.bfloat16)
    expert_count = gate_up.shape[0]
    local_experts = max(1, expert_count // half_size)
    copies = max(1, half_size // expert_count)

    def owner_major(weights):
        per_half = jnp.repeat(weights, copies, axis=0).reshape(
            (half_size, local_experts) + weights.shape[1:]
        )
        both = jnp.broadcast_to(per_half[None], (halves,) + per_half.shape)
        return both.reshape((group_count, local_experts) + weights.shape[1:])

    gu_rows = gate_up.shape[1]
    owned = lax.all_to_all(
        jnp.concatenate([owner_major(gate_up), owner_major(down_weight)], axis=2),
        dp, split_axis=0, concat_axis=0, tiled=True,
    )
    owned_gu = jnp.moveaxis(owned[:, :, :gu_rows], 0, 1).reshape(
        (1, local_experts, -1) + gate_up.shape[2:]
    )
    owned_dn = jnp.moveaxis(owned[:, :, gu_rows:], 0, 1).reshape(
        (1, local_experts, -1) + down_weight.shape[2:]
    )
    full_gu, full_dn = (
        lax.all_gather(owned_gu, "mp", axis=3, tiled=True),
        lax.all_gather(owned_dn, "mp", axis=3, tiled=True),
    )
    full_gu = full_gu[0]
    full_dn = full_dn[0]
    topk = routes.shape[1]
    capacity = 4 * ((rows_dev * topk + 3 * expert_count - 1) // (3 * expert_count))
    expert_ids = jnp.arange(expert_count, dtype=jnp.int32)
    hits = routes[:, :, None] == expert_ids[None, None, :]
    chosen = jnp.any(hits, axis=1)
    weight = jnp.sum(jnp.where(hits, route_gates.astype(jnp.float32)[:, :, None], 0.0), axis=1)
    rank = jnp.cumsum(chosen.astype(jnp.int32), axis=0) - 1
    slot_range = jnp.arange(capacity, dtype=jnp.int32)
    placed = chosen.T[:, None, :] & (rank.T[:, None, :] == slot_range[None, :, None])
    combine_table = (placed.astype(jnp.float32) * weight.T[:, None, :]).astype(jnp.bfloat16)
    halfway = full_gu.shape[-1] // 2
    if copies > 1:
        chunks = [(slice(None), 0)]
    else:
        chunks = [(slice(l, None, local_experts), l) for l in range(local_experts)]
    moe_sum = jnp.zeros((rows_dev, width), jnp.float32)
    for picked, l in chunks:
        table = placed[picked].astype(jnp.bfloat16)
        outbound = jnp.einsum(
            "ecr,rd->ecd", table, normed_moe, preferred_element_type=jnp.float32
        ).astype(jnp.bfloat16)
        outbound = outbound.reshape(half_size, -1, width)
        arrived = lax.all_to_all(outbound, DL, split_axis=0, concat_axis=0, tiled=True)
        both = jnp.einsum(
            "snd,df->snf", arrived, full_gu[l], preferred_element_type=jnp.float32
        )
        activation = (jax.nn.silu(both[..., :halfway]) * both[..., halfway:]).astype(jnp.bfloat16)
        expert_out = jnp.einsum(
            "snf,fd->snd", activation, full_dn[l], preferred_element_type=jnp.float32
        ).astype(jnp.bfloat16)
        returned = lax.all_to_all(expert_out, DL, split_axis=0, concat_axis=0, tiled=True)
        returned = returned.reshape(-1, capacity, width)
        moe_sum = moe_sum + jnp.einsum(
            "ecr,ecd->rd", combine_table[picked], returned, preferred_element_type=jnp.float32
        )
    return (residual + moe_sum).astype(jnp.bfloat16)


def solution(mesh):
    groups = mesh.shape["dp"]
    halves = 2 if groups % 2 == 0 else 1
    cores = 2 if groups % (2 * halves) == 0 else 1
    devices = mesh.devices.reshape(halves, groups // halves // cores, cores, mesh.shape["mp"])
    split_mesh = jax.sharding.Mesh(devices, ("zh", "dc", "core", "mp"))
    dp = ("zh", *DL)
    return jax.shard_map(
        local,
        mesh=split_mesh,
        in_specs=(
            P((*dp, "mp"), None),
            P((*dp, "mp"), None),
            P(),
            P(dp),
            P(dp),
            P("mp", dp, None, None),
            P("mp", dp, None, None),
            P(),
            P(),
            P(dp, "mp"),
            P("mp", dp),
            P(None, dp, "mp"),
            P(None, dp, "mp"),
            P((*dp, "mp"), None),
            P((*dp, "mp"), None),
        ),
        out_specs=P((*dp, "mp"), None),
        check_vma=False,
    )
```

```python
import jax
import jax.numpy as jnp
from jax import lax
from jax.sharding import PartitionSpec as P

EPSILON = 1e-06
ROTARY_BASE = 10000.0
SCORE_SCALE = 0.015625


def root_norm(values, gain):
    mean_square = jnp.mean(values * values, axis=-1, keepdims=True)
    return values * lax.rsqrt(mean_square + EPSILON) * gain


def rotary(vectors, positions):
    halfway = vectors.shape[-1] // 2
    freq_table = ROTARY_BASE ** (-jnp.arange(halfway).astype(jnp.float32) / halfway)
    angles = positions[..., None] * freq_table
    cosine = jnp.cos(angles)
    sine_part = jnp.sin(angles)
    leading = vectors[..., :halfway]
    trailing = vectors[..., halfway:]
    return jnp.concatenate(
        [leading * cosine - trailing * sine_part, trailing * cosine + leading * sine_part], axis=-1
    )


def split_heads(projected, positions, head_dim):
    per_group = projected.shape[-1] // head_dim - 2
    row_count = projected.shape[0]
    group_count = projected.shape[1]
    queries = projected[..., : per_group * head_dim].reshape(
        row_count, group_count, per_group, head_dim
    )
    key_rows = projected[..., per_group * head_dim : (per_group + 1) * head_dim]
    value_rows = projected[..., (per_group + 1) * head_dim :]
    queries = rotary(queries, positions[:, None, None]).astype(jnp.bfloat16)
    key_rows = rotary(key_rows, positions[:, None]).astype(jnp.bfloat16)
    return (queries, key_rows, value_rows.astype(jnp.bfloat16))


def prefill_attention(queries, key_rows, value_rows, prior, offset):
    head_dim = queries.shape[-1]
    row_count = queries.shape[0]
    span = prior.shape[1]
    all_keys = jnp.concatenate([prior[:, :, :head_dim], jnp.swapaxes(key_rows, 0, 1)], axis=1)
    all_values = jnp.concatenate([prior[:, :, head_dim:], jnp.swapaxes(value_rows, 0, 1)], axis=1)
    scores = (
        jnp.einsum("cgph,gkh->gpck", queries, all_keys, preferred_element_type=jnp.float32)
        * SCORE_SCALE
    )
    column = jnp.arange(span + row_count)
    row_ids = jnp.arange(row_count)
    allowed = jnp.where(
        column[None, :] < span, column[None, :] < offset, column[None, :] - span <= row_ids[:, None]
    )
    scores = jnp.where(allowed, scores, -jnp.inf)
    highest = jnp.max(scores, axis=-1, keepdims=True)
    expo = jnp.exp(scores - highest)
    weights = (expo / jnp.sum(expo, axis=-1, keepdims=True)).astype(jnp.bfloat16)
    mixed = jnp.einsum("gpck,gkh->cgph", weights, all_values, preferred_element_type=jnp.float32)
    return mixed.astype(jnp.bfloat16)


def decode_attention(queries, key_rows, value_rows, cache, lengths):
    head_dim = queries.shape[-1]
    cached = (
        jnp.einsum(
            "sgph,gslh->sgpl", queries, cache[..., :head_dim], preferred_element_type=jnp.float32
        )
        * SCORE_SCALE
    )
    own_score = (
        jnp.einsum("sgph,sgh->sgp", queries, key_rows, preferred_element_type=jnp.float32)
        * SCORE_SCALE
    )
    valid = jnp.arange(cache.shape[2])[None, :] < lengths[:, None]
    cached = jnp.where(valid[:, None, None, :], cached, -jnp.inf)
    highest = jnp.maximum(jnp.max(cached, axis=-1), own_score)
    expo = jnp.exp(cached - highest[..., None])
    own_expo = jnp.exp(own_score - highest)
    total = jnp.sum(expo, axis=-1) + own_expo
    weights = (expo / total[..., None]).astype(jnp.bfloat16)
    own_weight = (own_expo / total).astype(jnp.bfloat16)
    mixed = jnp.einsum(
        "sgpl,gslh->sgph", weights, cache[..., head_dim:], preferred_element_type=jnp.float32
    )
    mixed = (
        mixed
        + own_weight.astype(jnp.float32)[..., None] * value_rows.astype(jnp.float32)[:, :, None, :]
    )
    return mixed.astype(jnp.bfloat16)


def group_attention(projected, prior, cache, lengths, offset, pre_rows, head_dim):
    part_count = projected.shape[0]
    pre_part = projected[:, :pre_rows].reshape((-1,) + projected.shape[2:])
    dec_part = projected[:, pre_rows:].reshape((-1,) + projected.shape[2:])
    pre_pos = (offset + jnp.arange(pre_part.shape[0], dtype=jnp.int32)).astype(jnp.float32)
    dec_pos = lengths.astype(jnp.float32)
    queries, key_rows, value_rows = split_heads(pre_part, pre_pos, head_dim)
    pre_out = prefill_attention(queries, key_rows, value_rows, prior, offset)
    queries, key_rows, value_rows = split_heads(dec_part, dec_pos, head_dim)
    dec_out = decode_attention(queries, key_rows, value_rows, cache, lengths)
    columns = pre_out.shape[1] * pre_out.shape[2] * pre_out.shape[3]
    pre_out = pre_out.reshape(part_count, pre_rows, columns)
    dec_out = dec_out.reshape(part_count, -1, columns)
    return jnp.concatenate([pre_out, dec_out], axis=1).reshape(-1, columns)


def across_halves(shard):
    halves = lax.axis_size("zh")
    if halves == 1:
        return shard[None]
    other = lax.ppermute(shard, "zh", [(0, 1), (1, 0)])
    first = lax.axis_index("zh") == 0
    return jnp.stack([jnp.where(first, shard, other), jnp.where(first, other, shard)])


def local(
    pre_tokens,
    dec_tokens,
    deal_slots,
    dec_lengths,
    pre_offsets,
    dec_cache,
    prior_cache,
    attn_gain,
    moe_gain,
    qkv_weight,
    out_weight,
    gate_up,
    down_weight,
    routes,
    route_gates,
):
    dp = ("zh", "dl")
    halves = lax.axis_size("zh")
    half_size = lax.axis_size("dl")
    group_count = halves * half_size
    part_count = lax.axis_size("mp")
    group_index = lax.axis_index("zh") * half_size + lax.axis_index("dl")
    part_index = lax.axis_index("mp")
    pre_rows = pre_tokens.shape[0]
    width = pre_tokens.shape[1]
    dec_rows = dec_tokens.shape[0]
    head_dim = dec_cache.shape[-1] // 2
    bundle = max(1, dec_rows // group_count)
    device = group_index * part_count + part_index
    position = jnp.arange(dec_rows, dtype=jnp.int32)
    own_deal = lax.dynamic_slice_in_dim(deal_slots, device * dec_rows, dec_rows, 0)
    target = own_deal // (part_count * dec_rows)
    group_ids = jnp.arange(group_count, dtype=jnp.int32)
    lane_ids = jnp.arange(bundle, dtype=jnp.int32)
    send_table = (
        (target[None, None, :] == group_ids[:, None, None])
        & (position[None, None, :] % bundle == lane_ids[None, :, None])
    ).astype(jnp.bfloat16)
    outgoing = jnp.einsum(
        "jbi,id->jbd", send_table, dec_tokens, preferred_element_type=jnp.float32
    ).astype(jnp.bfloat16)
    incoming = lax.all_to_all(outgoing, dp, split_axis=0, concat_axis=0, tiled=True)
    slot_ids = device * dec_rows + position
    request_ids = jnp.arange(deal_slots.shape[0], dtype=jnp.int32)
    request = jnp.sum(
        jnp.where(deal_slots[None, :] == slot_ids[:, None], request_ids[None, :], 0), axis=1
    )
    source = request // (part_count * dec_rows)
    lane = request % dec_rows % bundle
    take_table = (
        (source[:, None, None] == group_ids[None, :, None])
        & (lane[:, None, None] == lane_ids[None, None, :])
    ).astype(jnp.bfloat16)
    slot_rows = jnp.einsum(
        "ijb,jbd->id", take_table, incoming, preferred_element_type=jnp.float32
    ).astype(jnp.bfloat16)
    expert_count = gate_up.shape[0]
    local_experts = max(1, expert_count // half_size)
    copies = max(1, half_size // expert_count)

    def owner_major(weights):
        per_half = jnp.repeat(weights, copies, axis=0).reshape(
            (half_size, local_experts) + weights.shape[1:]
        )
        both = jnp.broadcast_to(per_half[None], (halves,) + per_half.shape)
        return both.reshape((group_count, local_experts) + weights.shape[1:])

    weight_rows = jnp.concatenate([owner_major(gate_up), owner_major(down_weight)], axis=2)
    slot_rows, weight_rows, routes, prior_cache, dec_cache = lax.optimization_barrier(
        (slot_rows, weight_rows, routes, prior_cache, dec_cache)
    )
    layer_input = jnp.concatenate([pre_tokens, slot_rows], axis=0)
    rows_dev = layer_input.shape[0]
    normed = root_norm(layer_input.astype(jnp.float32), attn_gain).astype(jnp.bfloat16)
    group_rows = lax.all_gather(normed, "mp", axis=0, tiled=True)
    local_width = qkv_weight.shape[1]
    qkv_pair = across_halves(qkv_weight)
    out_pair = jnp.moveaxis(across_halves(out_weight), 0, 1)
    qkv_full = lax.all_gather(qkv_pair, "dl", axis=0, tiled=False)
    qkv_full = jnp.swapaxes(qkv_full, 0, 1).reshape(-1, local_width)
    qkv_full, out_pair = lax.optimization_barrier((qkv_full, out_pair))
    projected = jnp.dot(group_rows, qkv_full, preferred_element_type=jnp.float32)
    local_groups = dec_cache.shape[0]
    projected = projected.reshape(part_count, rows_dev, local_groups, local_width // local_groups)
    attn_out = group_attention(
        projected, prior_cache[:, 0], dec_cache, dec_lengths, pre_offsets[0], pre_rows, head_dim
    )
    out_full = lax.all_gather(out_pair, "dl", axis=1, tiled=False)
    out_full = jnp.swapaxes(out_full, 1, 2).reshape(out_weight.shape[0], -1)
    partial_sums = jnp.dot(attn_out, out_full, preferred_element_type=jnp.float32)
    attn_sum = lax.psum_scatter(
        partial_sums.astype(jnp.bfloat16), "mp", scatter_dimension=0, tiled=True
    ).astype(jnp.float32)
    residual = layer_input.astype(jnp.float32) + attn_sum
    normed_moe = root_norm(residual, moe_gain).astype(jnp.bfloat16)
    gu_rows = gate_up.shape[1]
    owned = lax.all_to_all(weight_rows, dp, split_axis=0, concat_axis=0, tiled=True)
    owned_gu = jnp.moveaxis(owned[:, :, :gu_rows], 0, 1).reshape(
        (1, local_experts, -1) + gate_up.shape[2:]
    )
    owned_dn = jnp.moveaxis(owned[:, :, gu_rows:], 0, 1).reshape(
        (1, local_experts, -1) + down_weight.shape[2:]
    )
    full_gu, full_dn = (
        lax.all_gather(owned_gu, "mp", axis=3, tiled=True),
        lax.all_gather(owned_dn, "mp", axis=3, tiled=True),
    )
    full_gu = full_gu[0]
    full_dn = full_dn[0]
    topk = routes.shape[1]
    capacity = 4 * ((rows_dev * topk + 3 * expert_count - 1) // (3 * expert_count))
    expert_ids = jnp.arange(expert_count, dtype=jnp.int32)
    hits = routes[:, :, None] == expert_ids[None, None, :]
    chosen = jnp.any(hits, axis=1)
    weight = jnp.sum(jnp.where(hits, route_gates.astype(jnp.float32)[:, :, None], 0.0), axis=1)
    rank = jnp.cumsum(chosen.astype(jnp.int32), axis=0) - 1
    slot_range = jnp.arange(capacity, dtype=jnp.int32)
    placed = chosen.T[:, None, :] & (rank.T[:, None, :] == slot_range[None, :, None])
    combine_table = (placed.astype(jnp.float32) * weight.T[:, None, :]).astype(jnp.bfloat16)
    halfway = full_gu.shape[-1] // 2
    if copies > 1:
        chunks = [(slice(None), 0)]
    else:
        chunks = [(slice(l, None, local_experts), l) for l in range(local_experts)]
    moe_sum = jnp.zeros((rows_dev, width), jnp.float32)
    for picked, l in chunks:
        table = placed[picked].astype(jnp.bfloat16)
        outbound = jnp.einsum(
            "ecr,rd->ecd", table, normed_moe, preferred_element_type=jnp.float32
        ).astype(jnp.bfloat16)
        outbound = outbound.reshape(half_size, -1, width)
        arrived = lax.all_to_all(outbound, "dl", split_axis=0, concat_axis=0, tiled=True)
        both = jnp.einsum(
            "snd,df->snf", arrived, full_gu[l], preferred_element_type=jnp.float32
        )
        activation = (jax.nn.silu(both[..., :halfway]) * both[..., halfway:]).astype(jnp.bfloat16)
        expert_out = jnp.einsum(
            "snf,fd->snd", activation, full_dn[l], preferred_element_type=jnp.float32
        ).astype(jnp.bfloat16)
        returned = lax.all_to_all(expert_out, "dl", split_axis=0, concat_axis=0, tiled=True)
        returned = returned.reshape(-1, capacity, width)
        moe_sum = moe_sum + jnp.einsum(
            "ecr,ecd->rd", combine_table[picked], returned, preferred_element_type=jnp.float32
        )
    return (residual + moe_sum).astype(jnp.bfloat16)


def solution(mesh):
    groups = mesh.shape["dp"]
    halves = 2 if groups % 2 == 0 else 1
    devices = mesh.devices.reshape(halves, groups // halves, mesh.shape["mp"])
    split_mesh = jax.sharding.Mesh(devices, ("zh", "dl", "mp"))
    dp = ("zh", "dl")
    return jax.shard_map(
        local,
        mesh=split_mesh,
        in_specs=(
            P((*dp, "mp"), None),
            P((*dp, "mp"), None),
            P(),
            P(dp),
            P(dp),
            P("mp", dp, None, None),
            P("mp", dp, None, None),
            P(),
            P(),
            P(dp, "mp"),
            P("mp", dp),
            P(None, dp, "mp"),
            P(None, dp, "mp"),
            P((*dp, "mp"), None),
            P((*dp, "mp"), None),
        ),
        out_specs=P((*dp, "mp"), None),
        check_vma=False,
    )
```

```python
import jax
import jax.numpy as jnp
from jax import lax
from jax.sharding import PartitionSpec as P

EPSILON = 1e-06
ROTARY_BASE = 10000.0
SCORE_SCALE = 0.015625


def root_norm(values, gain):
    mean_square = jnp.mean(values * values, axis=-1, keepdims=True)
    return values * lax.rsqrt(mean_square + EPSILON) * gain


def rotary(vectors, positions):
    halfway = vectors.shape[-1] // 2
    freq_table = ROTARY_BASE ** (-jnp.arange(halfway).astype(jnp.float32) / halfway)
    angles = positions[..., None] * freq_table
    cosine = jnp.cos(angles)
    sine_part = jnp.sin(angles)
    leading = vectors[..., :halfway]
    trailing = vectors[..., halfway:]
    return jnp.concatenate(
        [leading * cosine - trailing * sine_part, trailing * cosine + leading * sine_part], axis=-1
    )


def split_heads(projected, positions, head_dim):
    per_group = projected.shape[-1] // head_dim - 2
    row_count = projected.shape[0]
    group_count = projected.shape[1]
    queries = projected[..., : per_group * head_dim].reshape(
        row_count, group_count, per_group, head_dim
    )
    key_rows = projected[..., per_group * head_dim : (per_group + 1) * head_dim]
    value_rows = projected[..., (per_group + 1) * head_dim :]
    queries = rotary(queries, positions[:, None, None]).astype(jnp.bfloat16)
    key_rows = rotary(key_rows, positions[:, None]).astype(jnp.bfloat16)
    return (queries, key_rows, value_rows.astype(jnp.bfloat16))


def prefill_attention(queries, key_rows, value_rows, prior, offset):
    head_dim = queries.shape[-1]
    row_count = queries.shape[0]
    span = prior.shape[1]
    all_keys = jnp.concatenate([prior[:, :, :head_dim], jnp.swapaxes(key_rows, 0, 1)], axis=1)
    all_values = jnp.concatenate([prior[:, :, head_dim:], jnp.swapaxes(value_rows, 0, 1)], axis=1)
    scores = (
        jnp.einsum("cgph,gkh->gpck", queries, all_keys, preferred_element_type=jnp.float32)
        * SCORE_SCALE
    )
    column = jnp.arange(span + row_count)
    row_ids = jnp.arange(row_count)
    allowed = jnp.where(
        column[None, :] < span, column[None, :] < offset, column[None, :] - span <= row_ids[:, None]
    )
    scores = jnp.where(allowed, scores, -jnp.inf)
    highest = jnp.max(scores, axis=-1, keepdims=True)
    expo = jnp.exp(scores - highest)
    weights = (expo / jnp.sum(expo, axis=-1, keepdims=True)).astype(jnp.bfloat16)
    mixed = jnp.einsum("gpck,gkh->cgph", weights, all_values, preferred_element_type=jnp.float32)
    return mixed.astype(jnp.bfloat16)


def decode_attention(queries, key_rows, value_rows, cache, lengths):
    head_dim = queries.shape[-1]
    cached = (
        jnp.einsum(
            "sgph,gslh->sgpl", queries, cache[..., :head_dim], preferred_element_type=jnp.float32
        )
        * SCORE_SCALE
    )
    own_score = (
        jnp.einsum("sgph,sgh->sgp", queries, key_rows, preferred_element_type=jnp.float32)
        * SCORE_SCALE
    )
    valid = jnp.arange(cache.shape[2])[None, :] < lengths[:, None]
    cached = jnp.where(valid[:, None, None, :], cached, -jnp.inf)
    highest = jnp.maximum(jnp.max(cached, axis=-1), own_score)
    expo = jnp.exp(cached - highest[..., None])
    own_expo = jnp.exp(own_score - highest)
    total = jnp.sum(expo, axis=-1) + own_expo
    weights = (expo / total[..., None]).astype(jnp.bfloat16)
    own_weight = (own_expo / total).astype(jnp.bfloat16)
    mixed = jnp.einsum(
        "sgpl,gslh->sgph", weights, cache[..., head_dim:], preferred_element_type=jnp.float32
    )
    mixed = (
        mixed
        + own_weight.astype(jnp.float32)[..., None] * value_rows.astype(jnp.float32)[:, :, None, :]
    )
    return mixed.astype(jnp.bfloat16)


def group_attention(projected, prior, cache, lengths, offset, pre_rows, head_dim):
    part_count = projected.shape[0]
    pre_part = projected[:, :pre_rows].reshape((-1,) + projected.shape[2:])
    dec_part = projected[:, pre_rows:].reshape((-1,) + projected.shape[2:])
    pre_pos = (offset + jnp.arange(pre_part.shape[0], dtype=jnp.int32)).astype(jnp.float32)
    dec_pos = lengths.astype(jnp.float32)
    queries, key_rows, value_rows = split_heads(pre_part, pre_pos, head_dim)
    pre_out = prefill_attention(queries, key_rows, value_rows, prior, offset)
    queries, key_rows, value_rows = split_heads(dec_part, dec_pos, head_dim)
    dec_out = decode_attention(queries, key_rows, value_rows, cache, lengths)
    columns = pre_out.shape[1] * pre_out.shape[2] * pre_out.shape[3]
    pre_out = pre_out.reshape(part_count, pre_rows, columns)
    dec_out = dec_out.reshape(part_count, -1, columns)
    return jnp.concatenate([pre_out, dec_out], axis=1).reshape(-1, columns)


def across_halves(shard):
    halves = lax.axis_size("zh")
    if halves == 1:
        return shard[None]
    other = lax.ppermute(shard, "zh", [(0, 1), (1, 0)])
    first = lax.axis_index("zh") == 0
    return jnp.stack([jnp.where(first, shard, other), jnp.where(first, other, shard)])


def local(
    pre_tokens,
    dec_tokens,
    deal_slots,
    dec_lengths,
    pre_offsets,
    dec_cache,
    prior_cache,
    attn_gain,
    moe_gain,
    qkv_weight,
    out_weight,
    gate_up,
    down_weight,
    routes,
    route_gates,
):
    dp = ("zh", "dl")
    halves = lax.axis_size("zh")
    half_size = lax.axis_size("dl")
    group_count = halves * half_size
    part_count = lax.axis_size("mp")
    group_index = lax.axis_index("zh") * half_size + lax.axis_index("dl")
    part_index = lax.axis_index("mp")
    pre_rows = pre_tokens.shape[0]
    width = pre_tokens.shape[1]
    dec_rows = dec_tokens.shape[0]
    head_dim = dec_cache.shape[-1] // 2
    bundle = max(1, dec_rows // group_count)
    device = group_index * part_count + part_index
    position = jnp.arange(dec_rows, dtype=jnp.int32)
    own_deal = lax.dynamic_slice_in_dim(deal_slots, device * dec_rows, dec_rows, 0)
    target = own_deal // (part_count * dec_rows)
    group_ids = jnp.arange(group_count, dtype=jnp.int32)
    lane_ids = jnp.arange(bundle, dtype=jnp.int32)
    send_table = (
        (target[None, None, :] == group_ids[:, None, None])
        & (position[None, None, :] % bundle == lane_ids[None, :, None])
    ).astype(jnp.bfloat16)
    outgoing = jnp.einsum(
        "jbi,id->jbd", send_table, dec_tokens, preferred_element_type=jnp.float32
    ).astype(jnp.bfloat16)
    incoming = lax.all_to_all(outgoing, dp, split_axis=0, concat_axis=0, tiled=True)
    slot_ids = device * dec_rows + position
    request_ids = jnp.arange(deal_slots.shape[0], dtype=jnp.int32)
    request = jnp.sum(
        jnp.where(deal_slots[None, :] == slot_ids[:, None], request_ids[None, :], 0), axis=1
    )
    source = request // (part_count * dec_rows)
    lane = request % dec_rows % bundle
    take_table = (
        (source[:, None, None] == group_ids[None, :, None])
        & (lane[:, None, None] == lane_ids[None, None, :])
    ).astype(jnp.bfloat16)
    slot_rows = jnp.einsum(
        "ijb,jbd->id", take_table, incoming, preferred_element_type=jnp.float32
    ).astype(jnp.bfloat16)
    expert_count = gate_up.shape[0]
    local_experts = max(1, expert_count // half_size)
    copies = max(1, half_size // expert_count)

    def owner_major(weights):
        per_half = jnp.repeat(weights, copies, axis=0).reshape(
            (half_size, local_experts) + weights.shape[1:]
        )
        both = jnp.broadcast_to(per_half[None], (halves,) + per_half.shape)
        return both.reshape((group_count, local_experts) + weights.shape[1:])

    weight_rows = jnp.concatenate([owner_major(gate_up), owner_major(down_weight)], axis=2)
    weight_rows, routes, prior_cache, dec_cache = lax.optimization_barrier(
        (weight_rows, routes, prior_cache, dec_cache)
    )
    slot_rows, weight_rows = lax.optimization_barrier((slot_rows, weight_rows))
    layer_input = jnp.concatenate([pre_tokens, slot_rows], axis=0)
    rows_dev = layer_input.shape[0]
    normed = root_norm(layer_input.astype(jnp.float32), attn_gain).astype(jnp.bfloat16)
    group_rows = lax.all_gather(normed, "mp", axis=0, tiled=True)
    local_width = qkv_weight.shape[1]
    qkv_pair = across_halves(qkv_weight)
    out_pair = jnp.moveaxis(across_halves(out_weight), 0, 1)
    qkv_full = lax.all_gather(qkv_pair, "dl", axis=0, tiled=False)
    qkv_full = jnp.swapaxes(qkv_full, 0, 1).reshape(-1, local_width)
    qkv_full, out_pair = lax.optimization_barrier((qkv_full, out_pair))
    projected = jnp.dot(group_rows, qkv_full, preferred_element_type=jnp.float32)
    local_groups = dec_cache.shape[0]
    projected = projected.reshape(part_count, rows_dev, local_groups, local_width // local_groups)
    attn_out = group_attention(
        projected, prior_cache[:, 0], dec_cache, dec_lengths, pre_offsets[0], pre_rows, head_dim
    )
    out_full = lax.all_gather(out_pair, "dl", axis=1, tiled=False)
    out_full = jnp.swapaxes(out_full, 1, 2).reshape(out_weight.shape[0], -1)
    partial_sums = jnp.dot(attn_out, out_full, preferred_element_type=jnp.float32)
    attn_sum = lax.psum_scatter(
        partial_sums.astype(jnp.bfloat16), "mp", scatter_dimension=0, tiled=True
    ).astype(jnp.float32)
    residual = layer_input.astype(jnp.float32) + attn_sum
    normed_moe = root_norm(residual, moe_gain).astype(jnp.bfloat16)
    gu_rows = gate_up.shape[1]
    owned = lax.all_to_all(weight_rows, dp, split_axis=0, concat_axis=0, tiled=True)
    owned_gu = jnp.moveaxis(owned[:, :, :gu_rows], 0, 1).reshape(
        (1, local_experts, -1) + gate_up.shape[2:]
    )
    owned_dn = jnp.moveaxis(owned[:, :, gu_rows:], 0, 1).reshape(
        (1, local_experts, -1) + down_weight.shape[2:]
    )
    full_gu, full_dn = (
        lax.all_gather(owned_gu, "mp", axis=3, tiled=True),
        lax.all_gather(owned_dn, "mp", axis=3, tiled=True),
    )
    full_gu = full_gu[0]
    full_dn = full_dn[0]
    topk = routes.shape[1]
    capacity = 4 * ((rows_dev * topk + 3 * expert_count - 1) // (3 * expert_count))
    expert_ids = jnp.arange(expert_count, dtype=jnp.int32)
    hits = routes[:, :, None] == expert_ids[None, None, :]
    chosen = jnp.any(hits, axis=1)
    weight = jnp.sum(jnp.where(hits, route_gates.astype(jnp.float32)[:, :, None], 0.0), axis=1)
    rank = jnp.cumsum(chosen.astype(jnp.int32), axis=0) - 1
    slot_range = jnp.arange(capacity, dtype=jnp.int32)
    placed = chosen.T[:, None, :] & (rank.T[:, None, :] == slot_range[None, :, None])
    combine_table = (placed.astype(jnp.float32) * weight.T[:, None, :]).astype(jnp.bfloat16)
    halfway = full_gu.shape[-1] // 2
    if copies > 1:
        chunks = [(slice(None), 0)]
    else:
        chunks = [(slice(l, None, local_experts), l) for l in range(local_experts)]
    moe_sum = jnp.zeros((rows_dev, width), jnp.float32)
    for picked, l in chunks:
        table = placed[picked].astype(jnp.bfloat16)
        outbound = jnp.einsum(
            "ecr,rd->ecd", table, normed_moe, preferred_element_type=jnp.float32
        ).astype(jnp.bfloat16)
        outbound = outbound.reshape(half_size, -1, width)
        arrived = lax.all_to_all(outbound, "dl", split_axis=0, concat_axis=0, tiled=True)
        both = jnp.einsum(
            "snd,df->snf", arrived, full_gu[l], preferred_element_type=jnp.float32
        )
        activation = (jax.nn.silu(both[..., :halfway]) * both[..., halfway:]).astype(jnp.bfloat16)
        expert_out = jnp.einsum(
            "snf,fd->snd", activation, full_dn[l], preferred_element_type=jnp.float32
        ).astype(jnp.bfloat16)
        returned = lax.all_to_all(expert_out, "dl", split_axis=0, concat_axis=0, tiled=True)
        returned = returned.reshape(-1, capacity, width)
        moe_sum = moe_sum + jnp.einsum(
            "ecr,ecd->rd", combine_table[picked], returned, preferred_element_type=jnp.float32
        )
    return (residual + moe_sum).astype(jnp.bfloat16)


def solution(mesh):
    groups = mesh.shape["dp"]
    halves = 2 if groups % 2 == 0 else 1
    devices = mesh.devices.reshape(halves, groups // halves, mesh.shape["mp"])
    split_mesh = jax.sharding.Mesh(devices, ("zh", "dl", "mp"))
    dp = ("zh", "dl")
    return jax.shard_map(
        local,
        mesh=split_mesh,
        in_specs=(
            P((*dp, "mp"), None),
            P((*dp, "mp"), None),
            P(),
            P(dp),
            P(dp),
            P("mp", dp, None, None),
            P("mp", dp, None, None),
            P(),
            P(),
            P(dp, "mp"),
            P("mp", dp),
            P(None, dp, "mp"),
            P(None, dp, "mp"),
            P((*dp, "mp"), None),
            P((*dp, "mp"), None),
        ),
        out_specs=P((*dp, "mp"), None),
        check_vma=False,
    )
```
